32 devices in a mesh: rep: 4 (over y, core), fsdp: 4 (over z), seq: 2 (over x).
Axes of the slice: x: 2, y: 2, z: 4, core: 2. Of those that a mesh axis runs over, the one named last changes fastest.
Arguments:
- tokens: bfloat16 [16, 1024, 1024], P(('rep', 'fsdp'), 'seq'), may hold values from -6 to 6
- positions: int32 [3, 16, 1024], P(None, ('rep', 'fsdp'), 'seq'), may hold values from 0 to 15
- input_gain: bfloat16 [1024], P('fsdp'), may hold values from 0.5 to 1.5
- input_shift: bfloat16 [1024], P('fsdp'), may hold values from -1.5 to 1.5
- joint_weight: bfloat16 [1024, 3072], P('fsdp'), may hold values from -0.1875 to 0.1875
- joint_bias: bfloat16 [3072], P('fsdp'), may hold values from -1.5 to 1.5
- output_weight: bfloat16 [1024, 1024], P('fsdp'), may hold values from -3 to 3
- output_bias: bfloat16 [1024], P('fsdp'), may hold values from -1.5 to 1.5
- middle_gain: bfloat16 [1024], P('fsdp'), may hold values from 0.5 to 1.5
- middle_shift: bfloat16 [1024], P('fsdp'), may hold values from -1.5 to 1.5
- expand_weight: bfloat16 [1024, 4096], P('fsdp'), may hold values from -0.1875 to 0.1875
- expand_bias: bfloat16 [4096], P('fsdp'), may hold values from -2.5 to 2.5
- reduce_weight: bfloat16 [4096, 1024], P('fsdp'), may hold values from -0.09375 to 0.09375
- reduce_bias: bfloat16 [1024], P('fsdp'), may hold values from -1.5 to 1.5
- cotangent: bfloat16 [16, 1024, 1024], P(('rep', 'fsdp'), 'seq'), may hold values from -6 to 6
Outputs:
- block_output: bfloat16 [16, 1024, 1024], P(('rep', 'fsdp'), 'seq')
- input_gradient: float32 [16, 1024, 1024], P(('rep', 'fsdp'), 'seq')
- input_gain_gradient: float32 [1024], P('fsdp')
- input_shift_gradient: float32 [1024], P('fsdp')
- joint_weight_gradient: float32 [1024, 3072], P('fsdp')
- joint_bias_gradient: float32 [3072], P('fsdp')
- output_weight_gradient: float32 [1024, 1024], P('fsdp')
- output_bias_gradient: float32 [1024], P('fsdp')
- middle_gain_gradient: float32 [1024], P('fsdp')
- middle_shift_gradient: float32 [1024], P('fsdp')
- expand_weight_gradient: float32 [1024, 4096], P('fsdp')
- expand_bias_gradient: float32 [4096], P('fsdp')
- reduce_weight_gradient: float32 [4096, 1024], P('fsdp')
- reduce_bias_gradient: float32 [1024], P('fsdp')
The draws below stay inside these ranges and needn't reach their ends.
All inputs are finite; a program needn't handle non-finite values.
Results may differ from the reference program's by a relative error of at most 0.018.
Values may be sent and summed in bfloat16 or wider, within the bound.
No kernel may reach another device: no remote copies, remote signals or barrier semaphores. Data moves between devices by JAX's collectives and lax.ppermute only.
A program may use at most 192 MiB of HBM per device.

```python
import jax
import jax.numpy as jnp
from jax import lax

D = 1024
HEADS = 16
HD = 64
FF = 4096
CLIP = 1024
CLIPS = 16


def plant(values, stream_key, low, largest):
    longest = values.shape.index(max(values.shape))
    spots = []
    for shift in (0, 1):
        where = [jax.random.randint(jax.random.fold_in(stream_key, axis), (), 0, length) for axis, length in enumerate(values.shape)]
        where[longest] = (where[longest] + shift) % values.shape[longest]
        spots.append(tuple(where))
    return values.at[spots[0]].set(low).at[spots[1]].set(largest)


def level_of(key, dims, split, least, top_value):
    def one(axis_at, blocks):
        heights = jax.random.uniform(jax.random.fold_in(jax.random.fold_in(key, 6), axis_at), (blocks,), jnp.float32, least / len(split), top_value / len(split))
        return jnp.repeat(jnp.exp(heights), dims[axis_at] // blocks).reshape((-1,) + (1,) * (len(dims) - axis_at - 1))

    loudness = one(*split[0])
    for cut in split[1:]:
        loudness = loudness * one(*cut)
    return loudness


def scatter_about(stream_key, extent, width, bound, cuts=(), kind=jnp.bfloat16):
    array = width * jax.random.normal(stream_key, extent, jnp.float32)
    if cuts:
        array = array * level_of(stream_key, extent, cuts, -0.22, 0.18)
    return jnp.clip(array, -bound, bound).astype(kind)


def setup_inputs(seed: int = 0) -> dict:
    arg_keys = jax.random.split(jax.random.key(seed), 16)
    tokens = scatter_about(arg_keys[0], (CLIPS, CLIP, D), 1.0, 6.0, ((0, 16), (1, 2)))
    positions = plant(jax.random.randint(arg_keys[1], (3, CLIPS, CLIP), 0, 16), jax.random.fold_in(arg_keys[1], 1), 0, 15).astype(jnp.int32)
    input_gain = jnp.clip(1.0 + 0.1 * jax.random.normal(arg_keys[2], (D,), jnp.float32), 0.5, 1.5).astype(jnp.bfloat16)
    input_shift = scatter_about(arg_keys[3], (D,), 0.3, 1.5, ((0, 4),))
    joint_weight = scatter_about(arg_keys[4], (D, 3 * D), D ** -0.5, 0.1875, ((0, 4),))
    joint_bias = scatter_about(arg_keys[5], (3 * D,), 0.3, 1.5, ((0, 4),))
    output_weight = scatter_about(arg_keys[6], (D, D), (max(4 * D // CLIP, 1)) ** -0.5, 3.0, ((0, 4),))
    output_bias = scatter_about(arg_keys[7], (D,), 0.3, 1.5, ((0, 4),))
    middle_gain = jnp.clip(1.0 + 0.1 * jax.random.normal(arg_keys[8], (D,), jnp.float32), 0.5, 1.5).astype(jnp.bfloat16)
    middle_shift = scatter_about(arg_keys[9], (D,), 0.3, 1.5, ((0, 4),))
    expand_weight = scatter_about(arg_keys[10], (D, FF), D ** -0.5, 0.1875, ((0, 4),))
    expand_bias = scatter_about(arg_keys[11], (FF,), 0.5, 2.5, ((0, 4),))
    reduce_weight = scatter_about(arg_keys[12], (FF, D), FF ** -0.5, 0.09375, ((0, 4),))
    reduce_bias = scatter_about(arg_keys[13], (D,), 0.3, 1.5, ((0, 4),))
    cotangent = scatter_about(arg_keys[14], (CLIPS, CLIP, D), 1.0, 6.0, ((0, 16), (1, 2)))
    return dict(tokens=tokens, positions=positions, input_gain=input_gain, input_shift=input_shift, joint_weight=joint_weight, joint_bias=joint_bias, output_weight=output_weight, output_bias=output_bias, middle_gain=middle_gain, middle_shift=middle_shift, expand_weight=expand_weight, expand_bias=expand_bias, reduce_weight=reduce_weight, reduce_bias=reduce_bias, cotangent=cotangent)


@jax.custom_vjp
def low(v):
    return lax.optimization_barrier(v.astype(jnp.bfloat16)).astype(jnp.float32)

@jax.custom_vjp
def low_back(v):
    return v

def low_keep(v):
    return (low(v), None)

def low_pass(kept, grad):
    return (grad,)

def back_keep(v):
    return (v, None)

def back_low(kept, grad):
    return (low(grad),)
low.defvjp(low_keep, low_pass)
low_back.defvjp(back_keep, back_low)
epsilon = 1e-06

def norm_rows(values, gains, shifts):
    average = lax.optimization_barrier(jnp.mean(values, axis=-1, keepdims=True))
    centred = values - average
    spread = lax.optimization_barrier(jnp.mean(centred * centred, axis=-1, keepdims=True))
    return centred * lax.rsqrt(spread + epsilon) * gains + shifts

def rotary_tables(positions):
    counter = jnp.arange(10).astype(jnp.float32)
    frequency = jnp.power(10000.0, -counter / 10.0)
    angles = positions.astype(jnp.float32)[:, :, None] * frequency
    angles = jnp.transpose(angles, (1, 0, 2))
    return (jnp.cos(angles), jnp.sin(angles))

def rotate(values, cosine_part, sine_part):
    length = values.shape[0]
    heads_count = values.shape[1]
    turned = values[:, :, :60].reshape(length, heads_count, 3, 2, 10)
    former = turned[:, :, :, 0, :]
    latter = turned[:, :, :, 1, :]
    cosine_wide = cosine_part[:, None, :, :]
    sine_wide = sine_part[:, None, :, :]
    new_former = former * cosine_wide - latter * sine_wide
    new_latter = latter * cosine_wide + former * sine_wide
    joined = jnp.stack([new_former, new_latter], axis=3).reshape(length, heads_count, 60)
    return jnp.concatenate([joined, values[:, :, 60:]], axis=2)

def forward(tokens, positions, input_gain, input_shift, joint_weight, joint_bias, output_weight, output_bias, middle_gain, middle_shift, expand_weight, expand_bias, reduce_weight, reduce_bias):
    highest = lax.Precision.HIGHEST
    length = tokens.shape[0]
    normed_in = low(norm_rows(tokens, input_gain, input_shift))
    projected = low_back(jnp.dot(normed_in, joint_weight, precision=highest) + joint_bias)
    cosine_part, sine_part = rotary_tables(positions)
    queries = low(rotate(projected[:, :D].reshape(length, HEADS, HD), cosine_part, sine_part))
    keys = low(rotate(projected[:, D:2 * D].reshape(length, HEADS, HD), cosine_part, sine_part))
    values = low(projected[:, 2 * D:].reshape(length, HEADS, HD))
    scores = low_back(jnp.einsum('qhd,khd->hqk', queries, keys, precision=highest) * 0.125)
    weights_soft = low(jax.nn.softmax(scores, axis=-1))
    mixed = jnp.einsum('hqk,khd->qhd', weights_soft, values, precision=highest).reshape(length, D)
    attended = low(low_back(mixed))
    residual_mid = tokens + low_back(jnp.dot(attended, output_weight, precision=highest) + output_bias)
    normed_mid = low(norm_rows(residual_mid, middle_gain, middle_shift))
    upper = low_back(jnp.dot(normed_mid, expand_weight, precision=highest) + expand_bias)
    hidden = low(jax.nn.gelu(upper, approximate=False))
    return residual_mid + low_back(jnp.dot(hidden, reduce_weight, precision=highest) + reduce_bias)

def reference(tokens, positions, input_gain, input_shift, joint_weight, joint_bias, output_weight, output_bias, middle_gain, middle_shift, expand_weight, expand_bias, reduce_weight, reduce_bias, cotangent):
    weights_all = tuple((entry.astype(jnp.float32) for entry in (input_gain, input_shift, joint_weight, joint_bias, output_weight, output_bias, middle_gain, middle_shift, expand_weight, expand_bias, reduce_weight, reduce_bias)))

    def clip_step(totals, inputs):
        clip_tokens, clip_positions, clip_cotangent = inputs

        def clip_forward(values, *params):
            return forward(values, clip_positions, *params)
        result, pullback = jax.vjp(clip_forward, clip_tokens.astype(jnp.float32), *weights_all)
        gradients = pullback(clip_cotangent.astype(jnp.float32))
        totals = tuple((total + extra for total, extra in zip(totals, gradients[1:])))
        return (totals, (result.astype(jnp.bfloat16), gradients[0]))
    start = tuple((jnp.zeros(entry.shape, jnp.float32) for entry in weights_all))
    totals, stacked = lax.scan(clip_step, start, (tokens, jnp.transpose(positions, (1, 0, 2)), cotangent))
    return (stacked[0], stacked[1], totals[0], totals[1], totals[2], totals[3], totals[4], totals[5], totals[6], totals[7], totals[8], totals[9], totals[10], totals[11])
```

```python
import jax
import jax.numpy as jnp
from jax import lax
from jax.sharding import PartitionSpec as P

epsilon = 1e-06
LEVEL = ("rep", "seq")


def norm_rows(values, gains, shifts):
    average = jnp.mean(values, axis=-1, keepdims=True)
    centred = values - average
    spread = jnp.mean(centred * centred, axis=-1, keepdims=True)
    return centred * lax.rsqrt(spread + epsilon) * gains + shifts


def rotary_tables(positions):
    counter = jnp.arange(10).astype(jnp.float32)
    frequency = jnp.power(10000.0, -counter / 10.0)
    angles = positions.astype(jnp.float32)[:, :, None] * frequency
    angles = jnp.transpose(angles, (1, 0, 2))
    return (jnp.cos(angles), jnp.sin(angles))


def rotate(values, cosine_part, sine_part):
    length = values.shape[0]
    heads_count = values.shape[1]
    turned = values[:, :, :60].reshape(length, heads_count, 3, 2, 10)
    former = turned[:, :, :, 0, :]
    latter = turned[:, :, :, 1, :]
    cosine_wide = cosine_part[:, None, :, :]
    sine_wide = sine_part[:, None, :, :]
    new_former = former * cosine_wide - latter * sine_wide
    new_latter = latter * cosine_wide + former * sine_wide
    joined = jnp.stack([new_former, new_latter], axis=3).reshape(length, heads_count, 60)
    return jnp.concatenate([joined, values[:, :, 60:]], axis=2)


def exact_gelu(values):
    return jax.nn.gelu(values, approximate=False)


def split_heads(block):
    return block.reshape(block.shape[0], block.shape[1] // 64, 64)


def group_scores(query_heads, key_heads):
    return (
        jnp.einsum("thd,shd->hts", query_heads, key_heads, preferred_element_type=jnp.float32)
        * 0.125
    )


def attend(inputs):
    query_block, key_block, value_block = inputs
    query_heads = split_heads(query_block)
    key_heads = split_heads(key_block)
    value_heads = split_heads(value_block)
    scores = group_scores(query_heads, key_heads)
    row_max = jnp.max(scores, axis=2, keepdims=True)
    raised = jnp.exp(scores - row_max)
    row_total = jnp.sum(raised, axis=2, keepdims=True)
    probs_low = (raised / row_total).astype(jnp.bfloat16)
    mixed = jnp.einsum("hts,shd->thd", probs_low, value_heads, preferred_element_type=jnp.float32)
    return (mixed.reshape(query_block.shape[0], -1), row_max, row_total)


def attend_back(inputs):
    query_block, key_block, value_block, grad_block, row_max, row_total = inputs
    query_heads = split_heads(query_block)
    key_heads = split_heads(key_block)
    value_heads = split_heads(value_block)
    grad_heads = split_heads(grad_block)
    scores = group_scores(query_heads, key_heads)
    probs = jnp.exp(scores - row_max) / row_total
    probs_low = probs.astype(jnp.bfloat16)
    grad_probs = jnp.einsum(
        "thd,shd->hts", grad_heads, value_heads, preferred_element_type=jnp.float32
    )
    value_grad = jnp.einsum(
        "hts,thd->shd", probs_low, grad_heads, preferred_element_type=jnp.float32
    )
    inner = jnp.sum(grad_probs * probs, axis=2, keepdims=True)
    grad_scores = (probs * (grad_probs - inner)).astype(jnp.bfloat16)
    query_grad = (
        jnp.einsum("hts,shd->thd", grad_scores, key_heads, preferred_element_type=jnp.float32)
        * 0.125
    )
    key_grad = (
        jnp.einsum("hts,thd->shd", grad_scores, query_heads, preferred_element_type=jnp.float32)
        * 0.125
    )
    return (
        query_grad.reshape(query_block.shape[0], -1),
        key_grad.reshape(key_block.shape[0], -1),
        value_grad.reshape(key_block.shape[0], -1),
    )


def make_comm(mesh):
    n_rep, n_fsdp, n_seq = mesh.shape["rep"], mesh.shape["fsdp"], mesh.shape["seq"]
    level = n_rep * n_seq
    bits = level.bit_length() - 1
    assert 1 << bits == level and n_seq & (n_seq - 1) == 0 and n_rep % 2 == 0
    x_bits = list(range(n_seq.bit_length() - 1))
    core_bit = len(x_bits)
    y_bits = list(range(core_bit + 1, bits))

    def level_index():
        return lax.axis_index("rep") * n_seq + lax.axis_index("seq")

    def flip(bit):
        return [(k, k ^ (1 << bit)) for k in range(level)]

    def gather(piece):
        k = level_index()
        blocks = [(piece, 0)]
        for bit in x_bits + y_bits + [core_bit]:
            blocks = blocks + [
                (lax.ppermute(block, LEVEL, flip(bit)), mask ^ (1 << bit)) for block, mask in blocks
            ]
        out = jnp.zeros((piece.shape[0], level) + piece.shape[1:], piece.dtype)
        for block, mask in blocks:
            out = lax.dynamic_update_slice_in_dim(out, block[:, None], k ^ mask, axis=1)
        return out

    def reduce(total):
        k = level_index()
        lead = total.shape[0]
        rest = total.shape[2:]
        acc = total.reshape((lead,) + (2,) * bits + rest)
        alive = list(range(bits - 1, -1, -1))
        for bit in [core_bit] + y_bits[::-1] + x_bits[::-1]:
            axis = 1 + alive.index(bit)
            mine = (k >> bit) & 1
            keep = lax.dynamic_index_in_dim(acc, mine, axis, keepdims=False)
            send = lax.dynamic_index_in_dim(acc, 1 - mine, axis, keepdims=False)
            recv = lax.ppermute(send.astype(jnp.bfloat16), LEVEL, flip(bit))
            acc = keep.astype(jnp.float32) + recv.astype(jnp.float32)
            alive.remove(bit)
        return acc

    def line_reduce(acc):
        i = lax.axis_index("fsdp")
        n = n_fsdp
        up = [(a, a + 1) for a in range(n - 1)]
        down = [(a, a - 1) for a in range(1, n)]
        from_below = jnp.zeros(acc.shape[1:], jnp.float32)
        from_above = jnp.zeros(acc.shape[1:], jnp.float32)
        for step in range(1, n):
            j_up = jnp.clip(i + n - step, 0, n - 1)
            j_down = jnp.clip(i - (n - step), 0, n - 1)
            send_up = lax.dynamic_index_in_dim(acc, j_up, 0, keepdims=False) + from_below
            send_down = lax.dynamic_index_in_dim(acc, j_down, 0, keepdims=False) + from_above
            from_below = lax.ppermute(send_up.astype(jnp.bfloat16), "fsdp", up).astype(jnp.float32)
            from_above = lax.ppermute(send_down.astype(jnp.bfloat16), "fsdp", down).astype(jnp.float32)
        return lax.dynamic_index_in_dim(acc, i, 0, keepdims=False) + from_below + from_above

    def gather_params(shards):
        widths = [s.size // level for s in shards]
        packed = jnp.concatenate([s.reshape(level, -1) for s in shards], axis=1)
        mine = lax.dynamic_index_in_dim(packed, level_index(), 0, keepdims=False)
        along = lax.all_gather(mine, "fsdp", axis=0, tiled=False)
        full = gather(along)
        outs = []
        at = 0
        for s, w in zip(shards, widths):
            part = full[:, :, at : at + w].reshape((n_fsdp * s.shape[0],) + s.shape[1:])
            outs.append(part)
            at += w
        return outs

    def reduce_params(terms):
        widths = [t.size // (n_fsdp * level) for t in terms]
        packed = jnp.concatenate(
            [t.astype(jnp.bfloat16).reshape(n_fsdp, level, -1) for t in terms], axis=2
        )
        acc = reduce(packed)
        share = line_reduce(acc).astype(jnp.bfloat16)
        full = gather(share[None])[0]
        outs = []
        at = 0
        for t, w in zip(terms, widths):
            outs.append(
                full[:, at : at + w].reshape((t.shape[0] // n_fsdp,) + t.shape[1:]).astype(jnp.float32)
            )
            at += w
        return outs

    return gather_params, reduce_params


def seq_swap(block, n_seq):
    if n_seq == 2:
        return lax.ppermute(block, "seq", [(0, 1), (1, 0)])
    raise NotImplementedError


def make_local(mesh):
    gather_params, reduce_params = make_comm(mesh)
    n_seq = mesh.shape["seq"]

    def local(
        tokens,
        positions,
        input_gain,
        input_shift,
        joint_weight,
        joint_bias,
        output_weight,
        output_bias,
        middle_gain,
        middle_shift,
        expand_weight,
        expand_bias,
        reduce_weight,
        reduce_bias,
        cotangent,
    ):
        g_in_gain, g_in_shift, g_joint, g_joint_bias = gather_params(
            [input_gain, input_shift, joint_weight, joint_bias]
        )
        g_out, g_out_bias, g_mid_gain, g_mid_shift = gather_params(
            [output_weight, output_bias, middle_gain, middle_shift]
        )
        g_expand, g_expand_bias = gather_params([expand_weight, expand_bias])
        g_reduce, g_reduce_bias = gather_params([reduce_weight, reduce_bias])

        row_count = tokens.shape[1]
        width = tokens.shape[2]
        head_count = width // 64
        per_group = min(4, head_count)
        group_count = head_count // per_group
        group_width = per_group * 64

        def to_groups(block):
            return jnp.transpose(block.reshape(block.shape[0], group_count, group_width), (1, 0, 2))

        def from_groups(block):
            return jnp.transpose(block, (1, 0, 2)).reshape(block.shape[1], width)

        residual_in = tokens[0].astype(jnp.float32)
        cosine_part, sine_part = rotary_tables(positions[:, 0, :])
        in_gain = g_in_gain.astype(jnp.float32)
        in_shift = g_in_shift.astype(jnp.float32)
        normed_in = norm_rows(residual_in, in_gain, in_shift).astype(jnp.bfloat16)
        projected = jnp.dot(normed_in, g_joint, preferred_element_type=jnp.float32) + g_joint_bias.astype(
            jnp.float32
        )
        queries = (
            rotate(projected[:, :width].reshape(row_count, head_count, 64), cosine_part, sine_part)
            .astype(jnp.bfloat16)
            .reshape(row_count, width)
        )
        keys = (
            rotate(
                projected[:, width : 2 * width].reshape(row_count, head_count, 64),
                cosine_part,
                sine_part,
            )
            .astype(jnp.bfloat16)
            .reshape(row_count, width)
        )
        values = projected[:, 2 * width :].astype(jnp.bfloat16)
        query_groups = to_groups(queries)
        key_mine = to_groups(keys)
        value_mine = to_groups(values)
        key_all = jnp.concatenate([key_mine, seq_swap(key_mine, n_seq)], axis=1)
        value_all = jnp.concatenate([value_mine, seq_swap(value_mine, n_seq)], axis=1)
        mixed, row_max, row_total = lax.map(attend, (query_groups, key_all, value_all))
        attended = from_groups(mixed).astype(jnp.bfloat16)
        residual_mid = residual_in + (
            jnp.dot(attended, g_out, preferred_element_type=jnp.float32) + g_out_bias.astype(jnp.float32)
        )
        mid_gain = g_mid_gain.astype(jnp.float32)
        mid_shift = g_mid_shift.astype(jnp.float32)
        normed_mid = norm_rows(residual_mid, mid_gain, mid_shift).astype(jnp.bfloat16)
        upper = jnp.dot(normed_mid, g_expand, preferred_element_type=jnp.float32) + g_expand_bias.astype(
            jnp.float32
        )
        hidden = exact_gelu(upper).astype(jnp.bfloat16)
        result = residual_mid + (
            jnp.dot(hidden, g_reduce, preferred_element_type=jnp.float32) + g_reduce_bias.astype(jnp.float32)
        )
        block_output = result.astype(jnp.bfloat16)[None]

        grad_low = cotangent[0]
        grad_out = grad_low.astype(jnp.float32)
        reduce_term = jnp.einsum("tf,td->fd", hidden, grad_low, preferred_element_type=jnp.float32)
        reduce_offset_term = jnp.sum(grad_out, axis=0)
        d_reduce, d_reduce_bias = reduce_params([reduce_term, reduce_offset_term])
        grad_hidden = jnp.einsum("td,fd->tf", grad_low, g_reduce, preferred_element_type=jnp.float32)
        gelu_pull = jax.vjp(exact_gelu, upper)[1]
        grad_upper = gelu_pull(grad_hidden)[0].astype(jnp.bfloat16)
        expand_term = jnp.einsum("td,tf->df", normed_mid, grad_upper, preferred_element_type=jnp.float32)
        expand_offset_term = jnp.sum(grad_upper.astype(jnp.float32), axis=0)
        d_expand, d_expand_bias = reduce_params([expand_term, expand_offset_term])
        grad_mid_norm = jnp.einsum("tf,df->td", grad_upper, g_expand, preferred_element_type=jnp.float32)
        middle_pull = jax.vjp(norm_rows, residual_mid, mid_gain, mid_shift)[1]
        grad_mid_in, middle_gain_term, middle_shift_term = middle_pull(grad_mid_norm)
        grad_resid = grad_out + grad_mid_in
        grad_branch = grad_resid.astype(jnp.bfloat16)
        output_term = jnp.einsum("td,te->de", attended, grad_branch, preferred_element_type=jnp.float32)
        output_offset_term = jnp.sum(grad_branch.astype(jnp.float32), axis=0)
        d_out, d_out_bias, d_mid_gain, d_mid_shift = reduce_params(
            [output_term, output_offset_term, middle_gain_term, middle_shift_term]
        )
        grad_attended = jnp.einsum(
            "te,de->td", grad_branch, g_out, preferred_element_type=jnp.float32
        ).astype(jnp.bfloat16)
        query_grad, key_grad, value_grad = lax.map(
            attend_back,
            (query_groups, key_all, value_all, to_groups(grad_attended), row_max, row_total),
        )
        half = row_count
        key_share = key_grad[:, :half] + seq_swap(
            key_grad[:, half:].astype(jnp.bfloat16), n_seq
        ).astype(jnp.float32)
        value_share = value_grad[:, :half] + seq_swap(
            value_grad[:, half:].astype(jnp.bfloat16), n_seq
        ).astype(jnp.float32)
        grad_query = rotate(
            from_groups(query_grad).reshape(row_count, head_count, 64), cosine_part, -sine_part
        ).reshape(row_count, width)
        grad_key = rotate(
            from_groups(key_share).reshape(row_count, head_count, 64), cosine_part, -sine_part
        ).reshape(row_count, width)
        grad_value = from_groups(value_share)
        grad_projected = jnp.concatenate([grad_query, grad_key, grad_value], axis=1).astype(jnp.bfloat16)
        joint_term = jnp.einsum("td,te->de", normed_in, grad_projected, preferred_element_type=jnp.float32)
        joint_offset_term = jnp.sum(grad_projected.astype(jnp.float32), axis=0)
        grad_in_norm = jnp.einsum("te,de->td", grad_projected, g_joint, preferred_element_type=jnp.float32)
        input_pull = jax.vjp(norm_rows, residual_in, in_gain, in_shift)[1]
        grad_first_in, input_gain_term, input_shift_term = input_pull(grad_in_norm)
        input_gradient = (grad_resid + grad_first_in)[None]
        d_in_gain, d_in_shift, d_joint, d_joint_bias = reduce_params(
            [input_gain_term, input_shift_term, joint_term, joint_offset_term]
        )
        return (
            block_output,
            input_gradient,
            d_in_gain,
            d_in_shift,
            d_joint,
            d_joint_bias,
            d_out,
            d_out_bias,
            d_mid_gain,
            d_mid_shift,
            d_expand,
            d_expand_bias,
            d_reduce,
            d_reduce_bias,
        )

    return local


def solution(mesh):
    return jax.shard_map(
        make_local(mesh),
        mesh=mesh,
        in_specs=(
            P(("rep", "fsdp"), "seq", None),
            P(None, ("rep", "fsdp"), "seq"),
            P("fsdp"),
            P("fsdp"),
            P("fsdp", None),
            P("fsdp"),
            P("fsdp", None),
            P("fsdp"),
            P("fsdp"),
            P("fsdp"),
            P("fsdp", None),
            P("fsdp"),
            P("fsdp", None),
            P("fsdp"),
            P(("rep", "fsdp"), "seq", None),
        ),
        out_specs=(
            P(("rep", "fsdp"), "seq", None),
            P(("rep", "fsdp"), "seq", None),
            P("fsdp"),
            P("fsdp"),
            P("fsdp", None),
            P("fsdp"),
            P("fsdp", None),
            P("fsdp"),
            P("fsdp"),
            P("fsdp"),
            P("fsdp", None),
            P("fsdp"),
            P("fsdp", None),
            P("fsdp"),
        ),
        check_vma=False,
    )
```

```python
import jax
import jax.numpy as jnp
from jax import lax
from jax.sharding import PartitionSpec as P

epsilon = 1e-06
LEVEL = ("rep", "seq")
LANES = 128


def norm_rows(values, gains, shifts):
    average = jnp.mean(values, axis=-1, keepdims=True)
    centred = values - average
    spread = jnp.mean(centred * centred, axis=-1, keepdims=True)
    return centred * lax.rsqrt(spread + epsilon) * gains + shifts


def rotary_tables(positions):
    counter = jnp.arange(10).astype(jnp.float32)
    frequency = jnp.power(10000.0, -counter / 10.0)
    angles = positions.astype(jnp.float32)[:, :, None] * frequency
    angles = jnp.transpose(angles, (1, 0, 2))
    return (jnp.cos(angles), jnp.sin(angles))


def rotate(values, cosine_part, sine_part):
    length = values.shape[0]
    heads_count = values.shape[1]
    turned = values[:, :, :60].reshape(length, heads_count, 3, 2, 10)
    former = turned[:, :, :, 0, :]
    latter = turned[:, :, :, 1, :]
    cosine_wide = cosine_part[:, None, :, :]
    sine_wide = sine_part[:, None, :, :]
    new_former = former * cosine_wide - latter * sine_wide
    new_latter = latter * cosine_wide + former * sine_wide
    joined = jnp.stack([new_former, new_latter], axis=3).reshape(length, heads_count, 60)
    return jnp.concatenate([joined, values[:, :, 60:]], axis=2)


def exact_gelu(values):
    return jax.nn.gelu(values, approximate=False)


def split_heads(block):
    return block.reshape(block.shape[0], block.shape[1] // 64, 64)


def group_scores(query_heads, key_heads):
    return (
        jnp.einsum("thd,shd->hts", query_heads, key_heads, preferred_element_type=jnp.float32)
        * 0.125
    )


def attend(inputs):
    query_block, key_block, value_block = inputs
    query_heads = split_heads(query_block)
    key_heads = split_heads(key_block)
    value_heads = split_heads(value_block)
    scores = group_scores(query_heads, key_heads)
    row_max = jnp.max(scores, axis=2, keepdims=True)
    raised = jnp.exp(scores - row_max)
    row_total = jnp.sum(raised, axis=2, keepdims=True)
    probs_low = (raised / row_total).astype(jnp.bfloat16)
    mixed = jnp.einsum("hts,shd->thd", probs_low, value_heads, preferred_element_type=jnp.float32)
    return (mixed.reshape(query_block.shape[0], -1), row_max, row_total)


def attend_back(inputs):
    query_block, key_block, value_block, grad_block, row_max, row_total = inputs
    query_heads = split_heads(query_block)
    key_heads = split_heads(key_block)
    value_heads = split_heads(value_block)
    grad_heads = split_heads(grad_block)
    scores = group_scores(query_heads, key_heads)
    probs = jnp.exp(scores - row_max) / row_total
    probs_low = probs.astype(jnp.bfloat16)
    grad_probs = jnp.einsum(
        "thd,shd->hts", grad_heads, value_heads, preferred_element_type=jnp.float32
    )
    value_grad = jnp.einsum(
        "hts,thd->shd", probs_low, grad_heads, preferred_element_type=jnp.float32
    )
    inner = jnp.sum(grad_probs * probs, axis=2, keepdims=True)
    grad_scores = (probs * (grad_probs - inner)).astype(jnp.bfloat16)
    query_grad = (
        jnp.einsum("hts,shd->thd", grad_scores, key_heads, preferred_element_type=jnp.float32)
        * 0.125
    )
    key_grad = (
        jnp.einsum("hts,thd->shd", grad_scores, query_heads, preferred_element_type=jnp.float32)
        * 0.125
    )
    return (
        query_grad.reshape(query_block.shape[0], -1),
        key_grad.reshape(key_block.shape[0], -1),
        value_grad.reshape(key_block.shape[0], -1),
    )


def make_comm(mesh):
    n_rep, n_fsdp, n_seq = mesh.shape["rep"], mesh.shape["fsdp"], mesh.shape["seq"]
    level = n_rep * n_seq
    bits = level.bit_length() - 1
    assert 1 << bits == level and n_seq & (n_seq - 1) == 0 and n_rep % 2 == 0
    x_bits = list(range(n_seq.bit_length() - 1))
    core_bit = len(x_bits)
    y_bits = list(range(core_bit + 1, bits))

    def level_index():
        return lax.axis_index("rep") * n_seq + lax.axis_index("seq")

    def flip(bit):
        return [(k, k ^ (1 << bit)) for k in range(level)]

    def gather(piece):
        k = level_index()
        blocks = [(piece, 0)]
        for bit in x_bits + y_bits + [core_bit]:
            blocks = blocks + [
                (lax.ppermute(block, LEVEL, flip(bit)), mask ^ (1 << bit)) for block, mask in blocks
            ]
        out = jnp.zeros((level,) + piece.shape, piece.dtype)
        for block, mask in blocks:
            out = lax.dynamic_update_slice_in_dim(out, block[None], k ^ mask, axis=0)
        return out

    def reduce(total):
        k = level_index()
        acc = total.reshape((2,) * bits + total.shape[1:])
        alive = list(range(bits - 1, -1, -1))
        for bit in [core_bit] + y_bits[::-1] + x_bits[::-1]:
            axis = alive.index(bit)
            mine = (k >> bit) & 1
            keep = lax.dynamic_index_in_dim(acc, mine, axis, keepdims=False)
            send = lax.dynamic_index_in_dim(acc, 1 - mine, axis, keepdims=False)
            recv = lax.ppermute(send.astype(jnp.bfloat16), LEVEL, flip(bit))
            acc = keep.astype(jnp.float32) + recv.astype(jnp.float32)
            alive.remove(bit)
        return acc

    def line_reduce(acc):
        i = lax.axis_index("fsdp")
        n = n_fsdp
        up = [(a, a + 1) for a in range(n - 1)]
        down = [(a, a - 1) for a in range(1, n)]
        from_below = jnp.zeros(acc.shape[1:], jnp.float32)
        from_above = jnp.zeros(acc.shape[1:], jnp.float32)
        for step in range(1, n):
            j_up = jnp.clip(i + n - step, 0, n - 1)
            j_down = jnp.clip(i - (n - step), 0, n - 1)
            send_up = lax.dynamic_index_in_dim(acc, j_up, 0, keepdims=False) + from_below
            send_down = lax.dynamic_index_in_dim(acc, j_down, 0, keepdims=False) + from_above
            from_below = lax.ppermute(send_up.astype(jnp.bfloat16), "fsdp", up).astype(jnp.float32)
            from_above = lax.ppermute(send_down.astype(jnp.bfloat16), "fsdp", down).astype(jnp.float32)
        return lax.dynamic_index_in_dim(acc, i, 0, keepdims=False) + from_below + from_above

    def widths_of(sizes):
        widths = [-(-size // (level * LANES)) * LANES for size in sizes]
        total = -(-sum(widths) // (8 * LANES)) * (8 * LANES)
        return widths, total

    def pack(parts, widths, total, lead):
        cols = [
            jnp.pad(p, ((0, 0), (0, 0), (0, w - p.shape[2]))) for p, w in zip(parts, widths)
        ]
        cols.append(jnp.zeros((lead, level, total - sum(widths)), parts[0].dtype))
        joined = jnp.concatenate(cols, axis=2)
        return jnp.transpose(joined, (1, 0, 2)).reshape(level, lead, total // LANES, LANES)

    def gather_params(shards):
        widths, total = widths_of([s.size for s in shards])
        packed = pack([s.reshape(1, level, -1) for s in shards], widths, total, 1)
        mine = lax.dynamic_index_in_dim(packed, level_index(), 0, keepdims=False)[0]
        along = lax.all_gather(mine, "fsdp", axis=0, tiled=False)
        full = gather(along).reshape(level, n_fsdp, total)
        outs = []
        at = 0
        for s, w in zip(shards, widths):
            used = s.size // level
            part = jnp.transpose(full[:, :, at : at + used], (1, 0, 2))
            outs.append(part.reshape((n_fsdp * s.shape[0],) + s.shape[1:]))
            at += w
        return outs

    def reduce_params(terms):
        widths, total = widths_of([t.size // n_fsdp for t in terms])
        packed = pack(
            [t.astype(jnp.bfloat16).reshape(n_fsdp, level, -1) for t in terms], widths, total, n_fsdp
        )
        acc = reduce(packed)
        share = line_reduce(acc).astype(jnp.bfloat16)
        full = gather(share).reshape(level, total)
        outs = []
        at = 0
        for t, w in zip(terms, widths):
            used = t.size // (n_fsdp * level)
            part = full[:, at : at + used]
            outs.append(part.reshape((t.shape[0] // n_fsdp,) + t.shape[1:]).astype(jnp.float32))
            at += w
        return outs

    return gather_params, reduce_params


def seq_swap(block, n_seq):
    if n_seq == 2:
        return lax.ppermute(block, "seq", [(0, 1), (1, 0)])
    raise NotImplementedError


def make_local(mesh):
    gather_params, reduce_params = make_comm(mesh)
    n_seq = mesh.shape["seq"]

    def local(
        tokens,
        positions,
        input_gain,
        input_shift,
        joint_weight,
        joint_bias,
        output_weight,
        output_bias,
        middle_gain,
        middle_shift,
        expand_weight,
        expand_bias,
        reduce_weight,
        reduce_bias,
        cotangent,
    ):
        g_in_gain, g_in_shift, g_joint, g_joint_bias = gather_params(
            [input_gain, input_shift, joint_weight, joint_bias]
        )
        g_out, g_out_bias, g_mid_gain, g_mid_shift = gather_params(
            [output_weight, output_bias, middle_gain, middle_shift]
        )
        g_expand, g_expand_bias = gather_params([expand_weight, expand_bias])
        g_reduce, g_reduce_bias = gather_params([reduce_weight, reduce_bias])

        row_count = tokens.shape[1]
        width = tokens.shape[2]
        head_count = width // 64
        per_group = min(4, head_count)
        group_count = head_count // per_group
        group_width = per_group * 64

        def to_groups(block):
            return jnp.transpose(block.reshape(block.shape[0], group_count, group_width), (1, 0, 2))

        def from_groups(block):
            return jnp.transpose(block, (1, 0, 2)).reshape(block.shape[1], width)

        residual_in = tokens[0].astype(jnp.float32)
        cosine_part, sine_part = rotary_tables(positions[:, 0, :])
        in_gain = g_in_gain.astype(jnp.float32)
        in_shift = g_in_shift.astype(jnp.float32)
        normed_in = norm_rows(residual_in, in_gain, in_shift).astype(jnp.bfloat16)
        projected = jnp.dot(normed_in, g_joint, preferred_element_type=jnp.float32) + g_joint_bias.astype(
            jnp.float32
        )
        queries = (
            rotate(projected[:, :width].reshape(row_count, head_count, 64), cosine_part, sine_part)
            .astype(jnp.bfloat16)
            .reshape(row_count, width)
        )
        keys = (
            rotate(
                projected[:, width : 2 * width].reshape(row_count, head_count, 64),
                cosine_part,
                sine_part,
            )
            .astype(jnp.bfloat16)
            .reshape(row_count, width)
        )
        values = projected[:, 2 * width :].astype(jnp.bfloat16)
        query_groups = to_groups(queries)
        key_mine = to_groups(keys)
        value_mine = to_groups(values)
        key_all = jnp.concatenate([key_mine, seq_swap(key_mine, n_seq)], axis=1)
        value_all = jnp.concatenate([value_mine, seq_swap(value_mine, n_seq)], axis=1)
        mixed, row_max, row_total = lax.map(attend, (query_groups, key_all, value_all))
        attended = from_groups(mixed).astype(jnp.bfloat16)
        residual_mid = residual_in + (
            jnp.dot(attended, g_out, preferred_element_type=jnp.float32) + g_out_bias.astype(jnp.float32)
        )
        mid_gain = g_mid_gain.astype(jnp.float32)
        mid_shift = g_mid_shift.astype(jnp.float32)
        normed_mid = norm_rows(residual_mid, mid_gain, mid_shift).astype(jnp.bfloat16)
        upper = jnp.dot(normed_mid, g_expand, preferred_element_type=jnp.float32) + g_expand_bias.astype(
            jnp.float32
        )
        hidden = exact_gelu(upper).astype(jnp.bfloat16)
        result = residual_mid + (
            jnp.dot(hidden, g_reduce, preferred_element_type=jnp.float32) + g_reduce_bias.astype(jnp.float32)
        )
        block_output = result.astype(jnp.bfloat16)[None]

        grad_low = cotangent[0]
        grad_out = grad_low.astype(jnp.float32)
        reduce_term = jnp.einsum("tf,td->fd", hidden, grad_low, preferred_element_type=jnp.float32)
        reduce_offset_term = jnp.sum(grad_out, axis=0)
        d_reduce, d_reduce_bias = reduce_params([reduce_term, reduce_offset_term])
        grad_hidden = jnp.einsum("td,fd->tf", grad_low, g_reduce, preferred_element_type=jnp.float32)
        gelu_pull = jax.vjp(exact_gelu, upper)[1]
        grad_upper = gelu_pull(grad_hidden)[0].astype(jnp.bfloat16)
        expand_term = jnp.einsum("td,tf->df", normed_mid, grad_upper, preferred_element_type=jnp.float32)
        expand_offset_term = jnp.sum(grad_upper.astype(jnp.float32), axis=0)
        d_expand, d_expand_bias = reduce_params([expand_term, expand_offset_term])
        grad_mid_norm = jnp.einsum("tf,df->td", grad_upper, g_expand, preferred_element_type=jnp.float32)
        middle_pull = jax.vjp(norm_rows, residual_mid, mid_gain, mid_shift)[1]
        grad_mid_in, middle_gain_term, middle_shift_term = middle_pull(grad_mid_norm)
        grad_resid = grad_out + grad_mid_in
        grad_branch = grad_resid.astype(jnp.bfloat16)
        output_term = jnp.einsum("td,te->de", attended, grad_branch, preferred_element_type=jnp.float32)
        output_offset_term = jnp.sum(grad_branch.astype(jnp.float32), axis=0)
        d_out, d_out_bias, d_mid_gain, d_mid_shift = reduce_params(
            [output_term, output_offset_term, middle_gain_term, middle_shift_term]
        )
        grad_attended = jnp.einsum(
            "te,de->td", grad_branch, g_out, preferred_element_type=jnp.float32
        ).astype(jnp.bfloat16)
        query_grad, key_grad, value_grad = lax.map(
            attend_back,
            (query_groups, key_all, value_all, to_groups(grad_attended), row_max, row_total),
        )
        half = row_count
        key_share = key_grad[:, :half] + seq_swap(
            key_grad[:, half:].astype(jnp.bfloat16), n_seq
        ).astype(jnp.float32)
        value_share = value_grad[:, :half] + seq_swap(
            value_grad[:, half:].astype(jnp.bfloat16), n_seq
        ).astype(jnp.float32)
        grad_query = rotate(
            from_groups(query_grad).reshape(row_count, head_count, 64), cosine_part, -sine_part
        ).reshape(row_count, width)
        grad_key = rotate(
            from_groups(key_share).reshape(row_count, head_count, 64), cosine_part, -sine_part
        ).reshape(row_count, width)
        grad_value = from_groups(value_share)
        grad_projected = jnp.concatenate([grad_query, grad_key, grad_value], axis=1).astype(jnp.bfloat16)
        joint_term = jnp.einsum("td,te->de", normed_in, grad_projected, preferred_element_type=jnp.float32)
        joint_offset_term = jnp.sum(grad_projected.astype(jnp.float32), axis=0)
        grad_in_norm = jnp.einsum("te,de->td", grad_projected, g_joint, preferred_element_type=jnp.float32)
        input_pull = jax.vjp(norm_rows, residual_in, in_gain, in_shift)[1]
        grad_first_in, input_gain_term, input_shift_term = input_pull(grad_in_norm)
        input_gradient = (grad_resid + grad_first_in)[None]
        d_in_gain, d_in_shift, d_joint, d_joint_bias = reduce_params(
            [input_gain_term, input_shift_term, joint_term, joint_offset_term]
        )
        return (
            block_output,
            input_gradient,
            d_in_gain,
            d_in_shift,
            d_joint,
            d_joint_bias,
            d_out,
            d_out_bias,
            d_mid_gain,
            d_mid_shift,
            d_expand,
            d_expand_bias,
            d_reduce,
            d_reduce_bias,
        )

    return local


def solution(mesh):
    return jax.shard_map(
        make_local(mesh),
        mesh=mesh,
        in_specs=(
            P(("rep", "fsdp"), "seq", None),
            P(None, ("rep", "fsdp"), "seq"),
            P("fsdp"),
            P("fsdp"),
            P("fsdp", None),
            P("fsdp"),
            P("fsdp", None),
            P("fsdp"),
            P("fsdp"),
            P("fsdp"),
            P("fsdp", None),
            P("fsdp"),
            P("fsdp", None),
            P("fsdp"),
            P(("rep", "fsdp"), "seq", None),
        ),
        out_specs=(
            P(("rep", "fsdp"), "seq", None),
            P(("rep", "fsdp"), "seq", None),
            P("fsdp"),
            P("fsdp"),
            P("fsdp", None),
            P("fsdp"),
            P("fsdp", None),
            P("fsdp"),
            P("fsdp"),
            P("fsdp"),
            P("fsdp", None),
            P("fsdp"),
            P("fsdp", None),
            P("fsdp"),
        ),
        check_vma=False,
    )
```

```python
import jax
import jax.numpy as jnp
from jax import lax
from jax.sharding import PartitionSpec as P

epsilon = 1e-06
LEVEL = ("rep", "seq")
LANES = 128


def norm_rows(values, gains, shifts):
    average = jnp.mean(values, axis=-1, keepdims=True)
    centred = values - average
    spread = jnp.mean(centred * centred, axis=-1, keepdims=True)
    return centred * lax.rsqrt(spread + epsilon) * gains + shifts


def rotary_tables(positions):
    counter = jnp.arange(10).astype(jnp.float32)
    frequency = jnp.power(10000.0, -counter / 10.0)
    angles = positions.astype(jnp.float32)[:, :, None] * frequency
    angles = jnp.transpose(angles, (1, 0, 2))
    return (jnp.cos(angles), jnp.sin(angles))


def rotate(values, cosine_part, sine_part):
    length = values.shape[0]
    heads_count = values.shape[1]
    turned = values[:, :, :60].reshape(length, heads_count, 3, 2, 10)
    former = turned[:, :, :, 0, :]
    latter = turned[:, :, :, 1, :]
    cosine_wide = cosine_part[:, None, :, :]
    sine_wide = sine_part[:, None, :, :]
    new_former = former * cosine_wide - latter * sine_wide
    new_latter = latter * cosine_wide + former * sine_wide
    joined = jnp.stack([new_former, new_latter], axis=3).reshape(length, heads_count, 60)
    return jnp.concatenate([joined, values[:, :, 60:]], axis=2)


def exact_gelu(values):
    return jax.nn.gelu(values, approximate=False)


def split_heads(block):
    return block.reshape(block.shape[0], block.shape[1] // 64, 64)


def group_scores(query_heads, key_heads):
    return (
        jnp.einsum("thd,shd->hts", query_heads, key_heads, preferred_element_type=jnp.float32)
        * 0.125
    )


def attend(inputs):
    query_block, key_block, value_block = inputs
    query_heads = split_heads(query_block)
    key_heads = split_heads(key_block)
    value_heads = split_heads(value_block)
    scores = group_scores(query_heads, key_heads)
    row_max = jnp.max(scores, axis=2, keepdims=True)
    raised = jnp.exp(scores - row_max)
    row_total = jnp.sum(raised, axis=2, keepdims=True)
    probs_low = (raised / row_total).astype(jnp.bfloat16)
    mixed = jnp.einsum("hts,shd->thd", probs_low, value_heads, preferred_element_type=jnp.float32)
    return (mixed.reshape(query_block.shape[0], -1), row_max, row_total)


def attend_back(inputs):
    query_block, key_block, value_block, grad_block, row_max, row_total = inputs
    query_heads = split_heads(query_block)
    key_heads = split_heads(key_block)
    value_heads = split_heads(value_block)
    grad_heads = split_heads(grad_block)
    scores = group_scores(query_heads, key_heads)
    probs = jnp.exp(scores - row_max) / row_total
    probs_low = probs.astype(jnp.bfloat16)
    grad_probs = jnp.einsum(
        "thd,shd->hts", grad_heads, value_heads, preferred_element_type=jnp.float32
    )
    value_grad = jnp.einsum(
        "hts,thd->shd", probs_low, grad_heads, preferred_element_type=jnp.float32
    )
    inner = jnp.sum(grad_probs * probs, axis=2, keepdims=True)
    grad_scores = (probs * (grad_probs - inner)).astype(jnp.bfloat16)
    query_grad = (
        jnp.einsum("hts,shd->thd", grad_scores, key_heads, preferred_element_type=jnp.float32)
        * 0.125
    )
    key_grad = (
        jnp.einsum("hts,thd->shd", grad_scores, query_heads, preferred_element_type=jnp.float32)
        * 0.125
    )
    return (
        query_grad.reshape(query_block.shape[0], -1),
        key_grad.reshape(key_block.shape[0], -1),
        value_grad.reshape(key_block.shape[0], -1),
    )


def make_comm(mesh):
    n_rep, n_fsdp, n_seq = mesh.shape["rep"], mesh.shape["fsdp"], mesh.shape["seq"]
    level = n_rep * n_seq
    bits = level.bit_length() - 1
    assert 1 << bits == level and n_seq & (n_seq - 1) == 0 and n_rep % 2 == 0
    x_bits = list(range(n_seq.bit_length() - 1))
    core_bit = len(x_bits)
    y_bits = list(range(core_bit + 1, bits))

    def level_index():
        return lax.axis_index("rep") * n_seq + lax.axis_index("seq")

    def flip(bit):
        return [(k, k ^ (1 << bit)) for k in range(level)]

    def gather(piece, lead):
        k = level_index()
        blocks = [(piece, 0)]
        for bit in x_bits + y_bits + [core_bit]:
            blocks = blocks + [
                (lax.ppermute(block, LEVEL, flip(bit)), mask ^ (1 << bit)) for block, mask in blocks
            ]
        out = jnp.zeros((lead, level) + piece.shape[1:], piece.dtype)
        for block, mask in blocks:
            out = lax.dynamic_update_slice_in_dim(out, block[:, None], k ^ mask, axis=1)
        return out

    def reduce(total):
        k = level_index()
        lead = total.shape[0]
        acc = total.reshape((lead,) + (2,) * bits + total.shape[2:])
        alive = list(range(bits - 1, -1, -1))
        for bit in [core_bit] + y_bits[::-1] + x_bits[::-1]:
            axis = 1 + alive.index(bit)
            mine = (k >> bit) & 1
            keep = lax.dynamic_index_in_dim(acc, mine, axis, keepdims=False)
            send = lax.dynamic_index_in_dim(acc, 1 - mine, axis, keepdims=False)
            recv = lax.ppermute(send.astype(jnp.bfloat16), LEVEL, flip(bit))
            acc = keep.astype(jnp.float32) + recv.astype(jnp.float32)
            alive.remove(bit)
        return acc

    def line_reduce(acc):
        i = lax.axis_index("fsdp")
        n = n_fsdp
        up = [(a, a + 1) for a in range(n - 1)]
        down = [(a, a - 1) for a in range(1, n)]
        from_below = jnp.zeros(acc.shape[1:], jnp.float32)
        from_above = jnp.zeros(acc.shape[1:], jnp.float32)
        for step in range(1, n):
            j_up = jnp.clip(i + n - step, 0, n - 1)
            j_down = jnp.clip(i - (n - step), 0, n - 1)
            send_up = lax.dynamic_index_in_dim(acc, j_up, 0, keepdims=False) + from_below
            send_down = lax.dynamic_index_in_dim(acc, j_down, 0, keepdims=False) + from_above
            from_below = lax.ppermute(send_up.astype(jnp.bfloat16), "fsdp", up).astype(jnp.float32)
            from_above = lax.ppermute(send_down.astype(jnp.bfloat16), "fsdp", down).astype(jnp.float32)
        return lax.dynamic_index_in_dim(acc, i, 0, keepdims=False) + from_below + from_above

    def gather_weight(shard):
        rows, cols = shard.shape
        pieces = shard.reshape(level, rows // level, cols)
        mine = lax.dynamic_index_in_dim(pieces, level_index(), 0, keepdims=False)
        along = lax.all_gather(mine, "fsdp", axis=0, tiled=False)
        return gather(along, n_fsdp).reshape(n_fsdp * rows, cols)

    def reduce_weight(term):
        rows, cols = term.shape
        per = rows // (n_fsdp * level)
        acc = reduce(term.astype(jnp.bfloat16).reshape(n_fsdp, level, per, cols))
        share = line_reduce(acc).astype(jnp.bfloat16)
        return gather(share[None], 1).reshape(rows // n_fsdp, cols).astype(jnp.float32)

    def gather_vectors(shards):
        packed = jnp.concatenate(shards)
        full = lax.all_gather(packed, "fsdp", axis=0, tiled=False)
        outs = []
        at = 0
        for s in shards:
            outs.append(full[:, at : at + s.shape[0]].reshape(-1))
            at += s.shape[0]
        return outs

    def reduce_vectors(terms):
        packed = jnp.concatenate(terms)
        total = lax.psum(packed, ("rep", "fsdp", "seq"))
        f = lax.axis_index("fsdp")
        outs = []
        at = 0
        for t in terms:
            own = t.shape[0] // n_fsdp
            outs.append(lax.dynamic_slice_in_dim(total, at + f * own, own))
            at += t.shape[0]
        return outs

    def gather_params(shards):
        return [gather_weight(s) if s.ndim == 2 else s for s in shards]

    def reduce_params(terms):
        return [reduce_weight(t) if t.ndim == 2 else t for t in terms]

    return gather_params, reduce_params, gather_vectors, reduce_vectors


def seq_swap(block, n_seq):
    if n_seq == 2:
        return lax.ppermute(block, "seq", [(0, 1), (1, 0)])
    raise NotImplementedError


def make_local(mesh):
    gather_params, reduce_params, gather_vectors, reduce_vectors = make_comm(mesh)
    n_seq = mesh.shape["seq"]

    def local(
        tokens,
        positions,
        input_gain,
        input_shift,
        joint_weight,
        joint_bias,
        output_weight,
        output_bias,
        middle_gain,
        middle_shift,
        expand_weight,
        expand_bias,
        reduce_weight,
        reduce_bias,
        cotangent,
    ):
        (
            g_in_gain,
            g_in_shift,
            g_joint_bias,
            g_out_bias,
            g_mid_gain,
            g_mid_shift,
            g_expand_bias,
            g_reduce_bias,
        ) = gather_vectors(
            [
                input_gain,
                input_shift,
                joint_bias,
                output_bias,
                middle_gain,
                middle_shift,
                expand_bias,
                reduce_bias,
            ]
        )
        g_joint, g_out, g_expand, g_reduce = gather_params(
            [joint_weight, output_weight, expand_weight, reduce_weight]
        )

        row_count = tokens.shape[1]
        width = tokens.shape[2]
        head_count = width // 64
        per_group = min(4, head_count)
        group_count = head_count // per_group
        group_width = per_group * 64

        def to_groups(block):
            return jnp.transpose(block.reshape(block.shape[0], group_count, group_width), (1, 0, 2))

        def from_groups(block):
            return jnp.transpose(block, (1, 0, 2)).reshape(block.shape[1], width)

        residual_in = tokens[0].astype(jnp.float32)
        cosine_part, sine_part = rotary_tables(positions[:, 0, :])
        in_gain = g_in_gain.astype(jnp.float32)
        in_shift = g_in_shift.astype(jnp.float32)
        normed_in = norm_rows(residual_in, in_gain, in_shift).astype(jnp.bfloat16)
        projected = jnp.dot(normed_in, g_joint, preferred_element_type=jnp.float32) + g_joint_bias.astype(
            jnp.float32
        )
        queries = (
            rotate(projected[:, :width].reshape(row_count, head_count, 64), cosine_part, sine_part)
            .astype(jnp.bfloat16)
            .reshape(row_count, width)
        )
        keys = (
            rotate(
                projected[:, width : 2 * width].reshape(row_count, head_count, 64),
                cosine_part,
                sine_part,
            )
            .astype(jnp.bfloat16)
            .reshape(row_count, width)
        )
        values = projected[:, 2 * width :].astype(jnp.bfloat16)
        query_groups = to_groups(queries)
        key_mine = to_groups(keys)
        value_mine = to_groups(values)
        key_all = jnp.concatenate([key_mine, seq_swap(key_mine, n_seq)], axis=1)
        value_all = jnp.concatenate([value_mine, seq_swap(value_mine, n_seq)], axis=1)
        mixed, row_max, row_total = lax.map(attend, (query_groups, key_all, value_all))
        attended = from_groups(mixed).astype(jnp.bfloat16)
        residual_mid = residual_in + (
            jnp.dot(attended, g_out, preferred_element_type=jnp.float32) + g_out_bias.astype(jnp.float32)
        )
        mid_gain = g_mid_gain.astype(jnp.float32)
        mid_shift = g_mid_shift.astype(jnp.float32)
        normed_mid = norm_rows(residual_mid, mid_gain, mid_shift).astype(jnp.bfloat16)
        upper = jnp.dot(normed_mid, g_expand, preferred_element_type=jnp.float32) + g_expand_bias.astype(
            jnp.float32
        )
        hidden = exact_gelu(upper).astype(jnp.bfloat16)
        result = residual_mid + (
            jnp.dot(hidden, g_reduce, preferred_element_type=jnp.float32) + g_reduce_bias.astype(jnp.float32)
        )
        block_output = result.astype(jnp.bfloat16)[None]

        grad_low = cotangent[0]
        grad_out = grad_low.astype(jnp.float32)
        reduce_term = jnp.einsum("tf,td->fd", hidden, grad_low, preferred_element_type=jnp.float32)
        reduce_offset_term = jnp.sum(grad_out, axis=0)
        (d_reduce,) = reduce_params([reduce_term])
        grad_hidden = jnp.einsum("td,fd->tf", grad_low, g_reduce, preferred_element_type=jnp.float32)
        gelu_pull = jax.vjp(exact_gelu, upper)[1]
        grad_upper = gelu_pull(grad_hidden)[0].astype(jnp.bfloat16)
        expand_term = jnp.einsum("td,tf->df", normed_mid, grad_upper, preferred_element_type=jnp.float32)
        expand_offset_term = jnp.sum(grad_upper.astype(jnp.float32), axis=0)
        (d_expand,) = reduce_params([expand_term])
        grad_mid_norm = jnp.einsum("tf,df->td", grad_upper, g_expand, preferred_element_type=jnp.float32)
        middle_pull = jax.vjp(norm_rows, residual_mid, mid_gain, mid_shift)[1]
        grad_mid_in, middle_gain_term, middle_shift_term = middle_pull(grad_mid_norm)
        grad_resid = grad_out + grad_mid_in
        grad_branch = grad_resid.astype(jnp.bfloat16)
        output_term = jnp.einsum("td,te->de", attended, grad_branch, preferred_element_type=jnp.float32)
        output_offset_term = jnp.sum(grad_branch.astype(jnp.float32), axis=0)
        (d_out,) = reduce_params([output_term])
        grad_attended = jnp.einsum(
            "te,de->td", grad_branch, g_out, preferred_element_type=jnp.float32
        ).astype(jnp.bfloat16)
        query_grad, key_grad, value_grad = lax.map(
            attend_back,
            (query_groups, key_all, value_all, to_groups(grad_attended), row_max, row_total),
        )
        half = row_count
        key_share = key_grad[:, :half] + seq_swap(
            key_grad[:, half:].astype(jnp.bfloat16), n_seq
        ).astype(jnp.float32)
        value_share = value_grad[:, :half] + seq_swap(
            value_grad[:, half:].astype(jnp.bfloat16), n_seq
        ).astype(jnp.float32)
        grad_query = rotate(
            from_groups(query_grad).reshape(row_count, head_count, 64), cosine_part, -sine_part
        ).reshape(row_count, width)
        grad_key = rotate(
            from_groups(key_share).reshape(row_count, head_count, 64), cosine_part, -sine_part
        ).reshape(row_count, width)
        grad_value = from_groups(value_share)
        grad_projected = jnp.concatenate([grad_query, grad_key, grad_value], axis=1).astype(jnp.bfloat16)
        joint_term = jnp.einsum("td,te->de", normed_in, grad_projected, preferred_element_type=jnp.float32)
        joint_offset_term = jnp.sum(grad_projected.astype(jnp.float32), axis=0)
        grad_in_norm = jnp.einsum("te,de->td", grad_projected, g_joint, preferred_element_type=jnp.float32)
        input_pull = jax.vjp(norm_rows, residual_in, in_gain, in_shift)[1]
        grad_first_in, input_gain_term, input_shift_term = input_pull(grad_in_norm)
        input_gradient = (grad_resid + grad_first_in)[None]
        (d_joint,) = reduce_params([joint_term])
        (
            d_in_gain,
            d_in_shift,
            d_joint_bias,
            d_out_bias,
            d_mid_gain,
            d_mid_shift,
            d_expand_bias,
            d_reduce_bias,
        ) = reduce_vectors(
            [
                input_gain_term,
                input_shift_term,
                joint_offset_term,
                output_offset_term,
                middle_gain_term,
                middle_shift_term,
                expand_offset_term,
                reduce_offset_term,
            ]
        )
        return (
            block_output,
            input_gradient,
            d_in_gain,
            d_in_shift,
            d_joint,
            d_joint_bias,
            d_out,
            d_out_bias,
            d_mid_gain,
            d_mid_shift,
            d_expand,
            d_expand_bias,
            d_reduce,
            d_reduce_bias,
        )

    return local


def solution(mesh):
    return jax.shard_map(
        make_local(mesh),
        mesh=mesh,
        in_specs=(
            P(("rep", "fsdp"), "seq", None),
            P(None, ("rep", "fsdp"), "seq"),
            P("fsdp"),
            P("fsdp"),
            P("fsdp", None),
            P("fsdp"),
            P("fsdp", None),
            P("fsdp"),
            P("fsdp"),
            P("fsdp"),
            P("fsdp", None),
            P("fsdp"),
            P("fsdp", None),
            P("fsdp"),
            P(("rep", "fsdp"), "seq", None),
        ),
        out_specs=(
            P(("rep", "fsdp"), "seq", None),
            P(("rep", "fsdp"), "seq", None),
            P("fsdp"),
            P("fsdp"),
            P("fsdp", None),
            P("fsdp"),
            P("fsdp", None),
            P("fsdp"),
            P("fsdp"),
            P("fsdp"),
            P("fsdp", None),
            P("fsdp"),
            P("fsdp", None),
            P("fsdp"),
        ),
        check_vma=False,
    )
```

```python
import jax
import jax.numpy as jnp
from jax import lax
from jax.sharding import PartitionSpec as P

epsilon = 1e-06
LEVEL = ("rep", "seq")
LANES = 128


def norm_rows(values, gains, shifts):
    average = jnp.mean(values, axis=-1, keepdims=True)
    centred = values - average
    spread = jnp.mean(centred * centred, axis=-1, keepdims=True)
    return centred * lax.rsqrt(spread + epsilon) * gains + shifts


def rotary_tables(positions):
    counter = jnp.arange(10).astype(jnp.float32)
    frequency = jnp.power(10000.0, -counter / 10.0)
    angles = positions.astype(jnp.float32)[:, :, None] * frequency
    angles = jnp.transpose(angles, (1, 0, 2))
    return (jnp.cos(angles), jnp.sin(angles))


def rotate(values, cosine_part, sine_part):
    length = values.shape[0]
    heads_count = values.shape[1]
    turned = values[:, :, :60].reshape(length, heads_count, 3, 2, 10)
    former = turned[:, :, :, 0, :]
    latter = turned[:, :, :, 1, :]
    cosine_wide = cosine_part[:, None, :, :]
    sine_wide = sine_part[:, None, :, :]
    new_former = former * cosine_wide - latter * sine_wide
    new_latter = latter * cosine_wide + former * sine_wide
    joined = jnp.stack([new_former, new_latter], axis=3).reshape(length, heads_count, 60)
    return jnp.concatenate([joined, values[:, :, 60:]], axis=2)


def exact_gelu(values):
    return jax.nn.gelu(values, approximate=False)


def split_heads(block):
    return block.reshape(block.shape[0], block.shape[1] // 64, 64)


def group_scores(query_heads, key_heads):
    return (
        jnp.einsum("thd,shd->hts", query_heads, key_heads, preferred_element_type=jnp.float32)
        * 0.125
    )


def attend(inputs):
    query_block, key_block, value_block = inputs
    query_heads = split_heads(query_block)
    key_heads = split_heads(key_block)
    value_heads = split_heads(value_block)
    scores = group_scores(query_heads, key_heads)
    row_max = jnp.max(scores, axis=2, keepdims=True)
    raised = jnp.exp(scores - row_max)
    row_total = jnp.sum(raised, axis=2, keepdims=True)
    probs_low = (raised / row_total).astype(jnp.bfloat16)
    mixed = jnp.einsum("hts,shd->thd", probs_low, value_heads, preferred_element_type=jnp.float32)
    return (mixed.reshape(query_block.shape[0], -1), row_max, row_total)


def attend_back(inputs):
    query_block, key_block, value_block, grad_block, row_max, row_total = inputs
    query_heads = split_heads(query_block)
    key_heads = split_heads(key_block)
    value_heads = split_heads(value_block)
    grad_heads = split_heads(grad_block)
    scores = group_scores(query_heads, key_heads)
    probs = jnp.exp(scores - row_max) / row_total
    probs_low = probs.astype(jnp.bfloat16)
    grad_probs = jnp.einsum(
        "thd,shd->hts", grad_heads, value_heads, preferred_element_type=jnp.float32
    )
    value_grad = jnp.einsum(
        "hts,thd->shd", probs_low, grad_heads, preferred_element_type=jnp.float32
    )
    inner = jnp.sum(grad_probs * probs, axis=2, keepdims=True)
    grad_scores = (probs * (grad_probs - inner)).astype(jnp.bfloat16)
    query_grad = (
        jnp.einsum("hts,shd->thd", grad_scores, key_heads, preferred_element_type=jnp.float32)
        * 0.125
    )
    key_grad = (
        jnp.einsum("hts,thd->shd", grad_scores, query_heads, preferred_element_type=jnp.float32)
        * 0.125
    )
    return (
        query_grad.reshape(query_block.shape[0], -1),
        key_grad.reshape(key_block.shape[0], -1),
        value_grad.reshape(key_block.shape[0], -1),
    )


def make_comm(mesh):
    n_rep, n_fsdp, n_seq = mesh.shape["rep"], mesh.shape["fsdp"], mesh.shape["seq"]
    level = n_rep * n_seq
    bits = level.bit_length() - 1
    assert 1 << bits == level and n_seq & (n_seq - 1) == 0 and n_rep % 2 == 0
    x_bits = list(range(n_seq.bit_length() - 1))
    core_bit = len(x_bits)
    y_bits = list(range(core_bit + 1, bits))

    def level_index():
        return lax.axis_index("rep") * n_seq + lax.axis_index("seq")

    def flip(bit):
        return [(k, k ^ (1 << bit)) for k in range(level)]

    def gather(pieces, lead):
        k = level_index()
        blocks = [(pieces, 0)]
        for bit in x_bits + y_bits + [core_bit]:
            blocks = blocks + [
                (lax.ppermute(block, LEVEL, flip(bit)), mask ^ (1 << bit)) for block, mask in blocks
            ]
        outs = []
        for slot, piece in enumerate(pieces):
            out = jnp.zeros((lead, level) + piece.shape[1:], piece.dtype)
            for block, mask in blocks:
                out = lax.dynamic_update_slice_in_dim(out, block[slot][:, None], k ^ mask, axis=1)
            outs.append(out)
        return outs

    def reduce(totals):
        k = level_index()
        accs = [t.reshape((t.shape[0],) + (2,) * bits + t.shape[2:]) for t in totals]
        alive = list(range(bits - 1, -1, -1))
        for bit in [core_bit] + y_bits[::-1] + x_bits[::-1]:
            axis = 1 + alive.index(bit)
            mine = (k >> bit) & 1
            keep = [lax.dynamic_index_in_dim(a, mine, axis, keepdims=False) for a in accs]
            send = [
                lax.dynamic_index_in_dim(a, 1 - mine, axis, keepdims=False).astype(jnp.bfloat16)
                for a in accs
            ]
            recv = lax.ppermute(send, LEVEL, flip(bit))
            accs = [a.astype(jnp.float32) + b.astype(jnp.float32) for a, b in zip(keep, recv)]
            alive.remove(bit)
        return accs

    def line_reduce(accs):
        i = lax.axis_index("fsdp")
        n = n_fsdp
        up = [(a, a + 1) for a in range(n - 1)]
        down = [(a, a - 1) for a in range(1, n)]
        from_below = [jnp.zeros(a.shape[1:], jnp.float32) for a in accs]
        from_above = [jnp.zeros(a.shape[1:], jnp.float32) for a in accs]
        for step in range(1, n):
            j_up = jnp.clip(i + n - step, 0, n - 1)
            j_down = jnp.clip(i - (n - step), 0, n - 1)
            send_up = [
                (lax.dynamic_index_in_dim(a, j_up, 0, keepdims=False) + b).astype(jnp.bfloat16)
                for a, b in zip(accs, from_below)
            ]
            send_down = [
                (lax.dynamic_index_in_dim(a, j_down, 0, keepdims=False) + b).astype(jnp.bfloat16)
                for a, b in zip(accs, from_above)
            ]
            from_below = [r.astype(jnp.float32) for r in lax.ppermute(send_up, "fsdp", up)]
            from_above = [r.astype(jnp.float32) for r in lax.ppermute(send_down, "fsdp", down)]
        return [
            lax.dynamic_index_in_dim(a, i, 0, keepdims=False) + b + c
            for a, b, c in zip(accs, from_below, from_above)
        ]

    def packed_length(lengths):
        return -(-sum(lengths) // level) * level

    def gather_weight(shard, vectors):
        rows, cols = shard.shape
        lengths = [v.shape[0] for v in vectors]
        total = packed_length(lengths)
        flat = jnp.pad(jnp.concatenate(vectors), (0, total - sum(lengths)))
        k = level_index()
        mine = lax.dynamic_index_in_dim(shard.reshape(level, rows // level, cols), k, 0, keepdims=False)
        mine_vec = lax.dynamic_index_in_dim(flat.reshape(level, total // level), k, 0, keepdims=False)
        along = lax.all_gather([mine, mine_vec], "fsdp", axis=0, tiled=False)
        full, full_vec = gather(along, n_fsdp)
        full_vec = full_vec.reshape(n_fsdp, total)
        outs = []
        at = 0
        for length in lengths:
            outs.append(full_vec[:, at : at + length].reshape(-1))
            at += length
        return full.reshape(n_fsdp * rows, cols), outs

    def reduce_weight_term(term, vectors):
        rows, cols = term.shape
        per = rows // (n_fsdp * level)
        lengths = [v.shape[0] // n_fsdp for v in vectors]
        total = packed_length(lengths)
        flat = jnp.concatenate([v.reshape(n_fsdp, -1) for v in vectors], axis=1)
        flat = jnp.pad(flat, ((0, 0), (0, total - sum(lengths))))
        accs = reduce(
            [
                term.astype(jnp.bfloat16).reshape(n_fsdp, level, per, cols),
                flat.astype(jnp.bfloat16).reshape(n_fsdp, level, total // level),
            ]
        )
        shares = [a.astype(jnp.bfloat16) for a in line_reduce(accs)]
        full, full_vec = gather([shares[0][None], shares[1][None]], 1)
        full_vec = full_vec.reshape(total).astype(jnp.float32)
        outs = []
        at = 0
        for length in lengths:
            outs.append(full_vec[at : at + length])
            at += length
        return full.reshape(rows // n_fsdp, cols).astype(jnp.float32), outs

    return gather_weight, reduce_weight_term


def seq_swap(block, n_seq):
    if n_seq == 2:
        return lax.ppermute(block, "seq", [(0, 1), (1, 0)])
    raise NotImplementedError


def make_local(mesh):
    gather_full, reduce_owned = make_comm(mesh)
    n_seq = mesh.shape["seq"]

    def local(
        tokens,
        positions,
        input_gain,
        input_shift,
        joint_weight,
        joint_bias,
        output_weight,
        output_bias,
        middle_gain,
        middle_shift,
        expand_weight,
        expand_bias,
        reduce_weight,
        reduce_bias,
        cotangent,
    ):
        g_joint, (g_in_gain, g_in_shift, g_joint_bias) = gather_full(
            joint_weight, [input_gain, input_shift, joint_bias]
        )
        g_out, (g_out_bias, g_mid_gain, g_mid_shift) = gather_full(
            output_weight, [output_bias, middle_gain, middle_shift]
        )
        g_expand, (g_expand_bias,) = gather_full(expand_weight, [expand_bias])
        g_reduce, (g_reduce_bias,) = gather_full(reduce_weight, [reduce_bias])

        row_count = tokens.shape[1]
        width = tokens.shape[2]
        head_count = width // 64
        per_group = min(4, head_count)
        group_count = head_count // per_group
        group_width = per_group * 64

        def to_groups(block):
            return jnp.transpose(block.reshape(block.shape[0], group_count, group_width), (1, 0, 2))

        def from_groups(block):
            return jnp.transpose(block, (1, 0, 2)).reshape(block.shape[1], width)

        residual_in = tokens[0].astype(jnp.float32)
        cosine_part, sine_part = rotary_tables(positions[:, 0, :])
        in_gain = g_in_gain.astype(jnp.float32)
        in_shift = g_in_shift.astype(jnp.float32)
        normed_in = norm_rows(residual_in, in_gain, in_shift).astype(jnp.bfloat16)
        projected = jnp.dot(normed_in, g_joint, preferred_element_type=jnp.float32) + g_joint_bias.astype(
            jnp.float32
        )
        queries = (
            rotate(projected[:, :width].reshape(row_count, head_count, 64), cosine_part, sine_part)
            .astype(jnp.bfloat16)
            .reshape(row_count, width)
        )
        keys = (
            rotate(
                projected[:, width : 2 * width].reshape(row_count, head_count, 64),
                cosine_part,
                sine_part,
            )
            .astype(jnp.bfloat16)
            .reshape(row_count, width)
        )
        values = projected[:, 2 * width :].astype(jnp.bfloat16)
        query_groups = to_groups(queries)
        key_mine = to_groups(keys)
        value_mine = to_groups(values)
        key_all = jnp.concatenate([key_mine, seq_swap(key_mine, n_seq)], axis=1)
        value_all = jnp.concatenate([value_mine, seq_swap(value_mine, n_seq)], axis=1)
        mixed, row_max, row_total = lax.map(attend, (query_groups, key_all, value_all))
        attended = from_groups(mixed).astype(jnp.bfloat16)
        residual_mid = residual_in + (
            jnp.dot(attended, g_out, preferred_element_type=jnp.float32) + g_out_bias.astype(jnp.float32)
        )
        mid_gain = g_mid_gain.astype(jnp.float32)
        mid_shift = g_mid_shift.astype(jnp.float32)
        normed_mid = norm_rows(residual_mid, mid_gain, mid_shift).astype(jnp.bfloat16)
        upper = jnp.dot(normed_mid, g_expand, preferred_element_type=jnp.float32) + g_expand_bias.astype(
            jnp.float32
        )
        hidden = exact_gelu(upper).astype(jnp.bfloat16)
        result = residual_mid + (
            jnp.dot(hidden, g_reduce, preferred_element_type=jnp.float32) + g_reduce_bias.astype(jnp.float32)
        )
        block_output = result.astype(jnp.bfloat16)[None]

        grad_low = cotangent[0]
        grad_out = grad_low.astype(jnp.float32)
        reduce_term = jnp.einsum("tf,td->fd", hidden, grad_low, preferred_element_type=jnp.float32)
        reduce_offset_term = jnp.sum(grad_out, axis=0)
        d_reduce, (d_reduce_bias,) = reduce_owned(reduce_term, [reduce_offset_term])
        grad_hidden = jnp.einsum("td,fd->tf", grad_low, g_reduce, preferred_element_type=jnp.float32)
        gelu_pull = jax.vjp(exact_gelu, upper)[1]
        grad_upper = gelu_pull(grad_hidden)[0].astype(jnp.bfloat16)
        expand_term = jnp.einsum("td,tf->df", normed_mid, grad_upper, preferred_element_type=jnp.float32)
        expand_offset_term = jnp.sum(grad_upper.astype(jnp.float32), axis=0)
        d_expand, (d_expand_bias,) = reduce_owned(expand_term, [expand_offset_term])
        grad_mid_norm = jnp.einsum("tf,df->td", grad_upper, g_expand, preferred_element_type=jnp.float32)
        middle_pull = jax.vjp(norm_rows, residual_mid, mid_gain, mid_shift)[1]
        grad_mid_in, middle_gain_term, middle_shift_term = middle_pull(grad_mid_norm)
        grad_resid = grad_out + grad_mid_in
        grad_branch = grad_resid.astype(jnp.bfloat16)
        output_term = jnp.einsum("td,te->de", attended, grad_branch, preferred_element_type=jnp.float32)
        output_offset_term = jnp.sum(grad_branch.astype(jnp.float32), axis=0)
        d_out, (d_out_bias, d_mid_gain, d_mid_shift) = reduce_owned(
            output_term, [output_offset_term, middle_gain_term, middle_shift_term]
        )
        grad_attended = jnp.einsum(
            "te,de->td", grad_branch, g_out, preferred_element_type=jnp.float32
        ).astype(jnp.bfloat16)
        query_grad, key_grad, value_grad = lax.map(
            attend_back,
            (query_groups, key_all, value_all, to_groups(grad_attended), row_max, row_total),
        )
        half = row_count
        key_share = key_grad[:, :half] + seq_swap(
            key_grad[:, half:].astype(jnp.bfloat16), n_seq
        ).astype(jnp.float32)
        value_share = value_grad[:, :half] + seq_swap(
            value_grad[:, half:].astype(jnp.bfloat16), n_seq
        ).astype(jnp.float32)
        grad_query = rotate(
            from_groups(query_grad).reshape(row_count, head_count, 64), cosine_part, -sine_part
        ).reshape(row_count, width)
        grad_key = rotate(
            from_groups(key_share).reshape(row_count, head_count, 64), cosine_part, -sine_part
        ).reshape(row_count, width)
        grad_value = from_groups(value_share)
        grad_projected = jnp.concatenate([grad_query, grad_key, grad_value], axis=1).astype(jnp.bfloat16)
        joint_term = jnp.einsum("td,te->de", normed_in, grad_projected, preferred_element_type=jnp.float32)
        joint_offset_term = jnp.sum(grad_projected.astype(jnp.float32), axis=0)
        grad_in_norm = jnp.einsum("te,de->td", grad_projected, g_joint, preferred_element_type=jnp.float32)
        input_pull = jax.vjp(norm_rows, residual_in, in_gain, in_shift)[1]
        grad_first_in, input_gain_term, input_shift_term = input_pull(grad_in_norm)
        input_gradient = (grad_resid + grad_first_in)[None]
        d_joint, (d_in_gain, d_in_shift, d_joint_bias) = reduce_owned(
            joint_term, [input_gain_term, input_shift_term, joint_offset_term]
        )
        return (
            block_output,
            input_gradient,
            d_in_gain,
            d_in_shift,
            d_joint,
            d_joint_bias,
            d_out,
            d_out_bias,
            d_mid_gain,
            d_mid_shift,
            d_expand,
            d_expand_bias,
            d_reduce,
            d_reduce_bias,
        )

    return local


def solution(mesh):
    return jax.shard_map(
        make_local(mesh),
        mesh=mesh,
        in_specs=(
            P(("rep", "fsdp"), "seq", None),
            P(None, ("rep", "fsdp"), "seq"),
            P("fsdp"),
            P("fsdp"),
            P("fsdp", None),
            P("fsdp"),
            P("fsdp", None),
            P("fsdp"),
            P("fsdp"),
            P("fsdp"),
            P("fsdp", None),
            P("fsdp"),
            P("fsdp", None),
            P("fsdp"),
            P(("rep", "fsdp"), "seq", None),
        ),
        out_specs=(
            P(("rep", "fsdp"), "seq", None),
            P(("rep", "fsdp"), "seq", None),
            P("fsdp"),
            P("fsdp"),
            P("fsdp", None),
            P("fsdp"),
            P("fsdp", None),
            P("fsdp"),
            P("fsdp"),
            P("fsdp"),
            P("fsdp", None),
            P("fsdp"),
            P("fsdp", None),
            P("fsdp"),
        ),
        check_vma=False,
    )
```

```python
import jax
import jax.numpy as jnp
from jax import lax
from jax.sharding import PartitionSpec as P

epsilon = 1e-06
LEVEL = ("rep", "seq")
LANES = 128


def norm_rows(values, gains, shifts):
    average = jnp.mean(values, axis=-1, keepdims=True)
    centred = values - average
    spread = jnp.mean(centred * centred, axis=-1, keepdims=True)
    return centred * lax.rsqrt(spread + epsilon) * gains + shifts


def rotary_tables(positions):
    counter = jnp.arange(10).astype(jnp.float32)
    frequency = jnp.power(10000.0, -counter / 10.0)
    angles = positions.astype(jnp.float32)[:, :, None] * frequency
    angles = jnp.transpose(angles, (1, 0, 2))
    return (jnp.cos(angles), jnp.sin(angles))


def rotate(values, cosine_part, sine_part):
    length = values.shape[0]
    heads_count = values.shape[1]
    turned = values[:, :, :60].reshape(length, heads_count, 3, 2, 10)
    former = turned[:, :, :, 0, :]
    latter = turned[:, :, :, 1, :]
    cosine_wide = cosine_part[:, None, :, :]
    sine_wide = sine_part[:, None, :, :]
    new_former = former * cosine_wide - latter * sine_wide
    new_latter = latter * cosine_wide + former * sine_wide
    joined = jnp.stack([new_former, new_latter], axis=3).reshape(length, heads_count, 60)
    return jnp.concatenate([joined, values[:, :, 60:]], axis=2)


def exact_gelu(values):
    return jax.nn.gelu(values, approximate=False)


def split_heads(block):
    return block.reshape(block.shape[0], block.shape[1] // 64, 64)


def group_scores(query_heads, key_heads):
    return (
        jnp.einsum("thd,shd->hts", query_heads, key_heads, preferred_element_type=jnp.float32)
        * 0.125
    )


def attend(inputs):
    query_block, key_block, value_block = inputs
    query_heads = split_heads(query_block)
    key_heads = split_heads(key_block)
    value_heads = split_heads(value_block)
    scores = group_scores(query_heads, key_heads)
    row_max = jnp.max(scores, axis=2, keepdims=True)
    raised = jnp.exp(scores - row_max)
    row_total = jnp.sum(raised, axis=2, keepdims=True)
    probs_low = (raised / row_total).astype(jnp.bfloat16)
    mixed = jnp.einsum("hts,shd->thd", probs_low, value_heads, preferred_element_type=jnp.float32)
    return (mixed.reshape(query_block.shape[0], -1), row_max, row_total)


def attend_back(inputs):
    query_block, key_block, value_block, grad_block, row_max, row_total = inputs
    query_heads = split_heads(query_block)
    key_heads = split_heads(key_block)
    value_heads = split_heads(value_block)
    grad_heads = split_heads(grad_block)
    scores = group_scores(query_heads, key_heads)
    probs = jnp.exp(scores - row_max) / row_total
    probs_low = probs.astype(jnp.bfloat16)
    grad_probs = jnp.einsum(
        "thd,shd->hts", grad_heads, value_heads, preferred_element_type=jnp.float32
    )
    value_grad = jnp.einsum(
        "hts,thd->shd", probs_low, grad_heads, preferred_element_type=jnp.float32
    )
    inner = jnp.sum(grad_probs * probs, axis=2, keepdims=True)
    grad_scores = (probs * (grad_probs - inner)).astype(jnp.bfloat16)
    query_grad = (
        jnp.einsum("hts,shd->thd", grad_scores, key_heads, preferred_element_type=jnp.float32)
        * 0.125
    )
    key_grad = (
        jnp.einsum("hts,thd->shd", grad_scores, query_heads, preferred_element_type=jnp.float32)
        * 0.125
    )
    return (
        query_grad.reshape(query_block.shape[0], -1),
        key_grad.reshape(key_block.shape[0], -1),
        value_grad.reshape(key_block.shape[0], -1),
    )


def make_comm(mesh):
    n_rep, n_fsdp, n_seq = mesh.shape["rep"], mesh.shape["fsdp"], mesh.shape["seq"]
    level = n_rep * n_seq
    bits = level.bit_length() - 1
    assert 1 << bits == level and n_seq & (n_seq - 1) == 0 and n_rep % 2 == 0
    x_bits = list(range(n_seq.bit_length() - 1))
    core_bit = len(x_bits)
    y_bits = list(range(core_bit + 1, bits))

    def level_index():
        return lax.axis_index("rep") * n_seq + lax.axis_index("seq")

    def flip(bit):
        return [(k, k ^ (1 << bit)) for k in range(level)]

    def gather(piece, lead, order=None):
        k = level_index()
        blocks = [(piece, 0)]
        for bit in order or (x_bits + y_bits + [core_bit]):
            blocks = blocks + [
                (lax.ppermute(block, LEVEL, flip(bit)), mask ^ (1 << bit)) for block, mask in blocks
            ]
        out = jnp.zeros((lead, level) + piece.shape[1:], piece.dtype)
        for block, mask in blocks:
            out = lax.dynamic_update_slice_in_dim(out, block[:, None], k ^ mask, axis=1)
        return out

    def reduce(total):
        k = level_index()
        lead = total.shape[0]
        acc = total.reshape((lead,) + (2,) * bits + total.shape[2:])
        alive = list(range(bits - 1, -1, -1))
        for bit in [core_bit] + y_bits[::-1] + x_bits[::-1]:
            axis = 1 + alive.index(bit)
            mine = (k >> bit) & 1
            keep = lax.dynamic_index_in_dim(acc, mine, axis, keepdims=False)
            send = lax.dynamic_index_in_dim(acc, 1 - mine, axis, keepdims=False)
            recv = lax.ppermute(send.astype(jnp.bfloat16), LEVEL, flip(bit))
            acc = keep.astype(jnp.float32) + recv.astype(jnp.float32)
            alive.remove(bit)
        return acc

    def line_reduce(acc):
        i = lax.axis_index("fsdp")
        n = n_fsdp
        up = [(a, a + 1) for a in range(n - 1)]
        down = [(a, a - 1) for a in range(1, n)]
        from_below = jnp.zeros(acc.shape[1:], jnp.float32)
        from_above = jnp.zeros(acc.shape[1:], jnp.float32)
        for step in range(1, n):
            j_up = jnp.clip(i + n - step, 0, n - 1)
            j_down = jnp.clip(i - (n - step), 0, n - 1)
            send_up = lax.dynamic_index_in_dim(acc, j_up, 0, keepdims=False) + from_below
            send_down = lax.dynamic_index_in_dim(acc, j_down, 0, keepdims=False) + from_above
            from_below = lax.ppermute(send_up.astype(jnp.bfloat16), "fsdp", up).astype(jnp.float32)
            from_above = lax.ppermute(send_down.astype(jnp.bfloat16), "fsdp", down).astype(jnp.float32)
        return lax.dynamic_index_in_dim(acc, i, 0, keepdims=False) + from_below + from_above

    def gather_weight(shard):
        rows, cols = shard.shape
        pieces = shard.reshape(level, rows // level, cols)
        mine = lax.dynamic_index_in_dim(pieces, level_index(), 0, keepdims=False)
        along = lax.all_gather(mine, "fsdp", axis=0, tiled=False)
        return gather(along, n_fsdp).reshape(n_fsdp * rows, cols)

    def reduce_weight(term):
        rows, cols = term.shape
        per = rows // (n_fsdp * level)
        acc = reduce(term.astype(jnp.bfloat16).reshape(n_fsdp, level, per, cols))
        share = line_reduce(acc).astype(jnp.bfloat16)
        return gather(share[None], 1).reshape(rows // n_fsdp, cols).astype(jnp.float32)

    def stage_one(term):
        rows, cols = term.shape
        per = rows // (n_fsdp * level)
        return reduce(term.astype(jnp.bfloat16).reshape(n_fsdp, level, per, cols))

    def stage_two(acc):
        return line_reduce(acc).astype(jnp.bfloat16)

    def stage_three(share):
        rows, cols = share.shape
        full = gather(share[None], 1, y_bits + x_bits + [core_bit])
        return full.reshape(level * rows, cols).astype(jnp.float32)

    def gather_vectors(shards):
        packed = jnp.concatenate(shards)
        full = lax.all_gather(packed, "fsdp", axis=0, tiled=False)
        outs = []
        at = 0
        for s in shards:
            outs.append(full[:, at : at + s.shape[0]].reshape(-1))
            at += s.shape[0]
        return outs

    def reduce_vectors(terms):
        packed = jnp.concatenate(terms)
        total = lax.psum(packed.astype(jnp.bfloat16), ("rep", "fsdp", "seq")).astype(jnp.float32)
        f = lax.axis_index("fsdp")
        outs = []
        at = 0
        for t in terms:
            own = t.shape[0] // n_fsdp
            outs.append(lax.dynamic_slice_in_dim(total, at + f * own, own))
            at += t.shape[0]
        return outs

    def gather_params(shards):
        return [gather_weight(s) if s.ndim == 2 else s for s in shards]

    def reduce_params(terms):
        return [reduce_weight(t) if t.ndim == 2 else t for t in terms]

    return gather_params, (stage_one, stage_two, stage_three), gather_vectors, reduce_vectors


def seq_swap(block, n_seq):
    if n_seq == 2:
        return lax.ppermute(block, "seq", [(0, 1), (1, 0)])
    raise NotImplementedError


def make_local(mesh):
    gather_params, stages, gather_vectors, reduce_vectors = make_comm(mesh)
    stage_one, stage_two, stage_three = stages
    n_seq = mesh.shape["seq"]

    def local(
        tokens,
        positions,
        input_gain,
        input_shift,
        joint_weight,
        joint_bias,
        output_weight,
        output_bias,
        middle_gain,
        middle_shift,
        expand_weight,
        expand_bias,
        reduce_weight,
        reduce_bias,
        cotangent,
    ):
        (
            g_in_gain,
            g_in_shift,
            g_joint_bias,
            g_out_bias,
            g_mid_gain,
            g_mid_shift,
            g_expand_bias,
            g_reduce_bias,
        ) = gather_vectors(
            [
                input_gain,
                input_shift,
                joint_bias,
                output_bias,
                middle_gain,
                middle_shift,
                expand_bias,
                reduce_bias,
            ]
        )
        g_joint, g_out, g_expand, g_reduce = gather_params(
            [joint_weight, output_weight, expand_weight, reduce_weight]
        )

        row_count = tokens.shape[1]
        width = tokens.shape[2]
        head_count = width // 64
        per_group = min(4, head_count)
        group_count = head_count // per_group
        group_width = per_group * 64

        def to_groups(block):
            return jnp.transpose(block.reshape(block.shape[0], group_count, group_width), (1, 0, 2))

        def from_groups(block):
            return jnp.transpose(block, (1, 0, 2)).reshape(block.shape[1], width)

        residual_in = tokens[0].astype(jnp.float32)
        cosine_part, sine_part = rotary_tables(positions[:, 0, :])
        in_gain = g_in_gain.astype(jnp.float32)
        in_shift = g_in_shift.astype(jnp.float32)
        normed_in = norm_rows(residual_in, in_gain, in_shift).astype(jnp.bfloat16)
        projected = jnp.dot(normed_in, g_joint, preferred_element_type=jnp.float32) + g_joint_bias.astype(
            jnp.float32
        )
        queries = (
            rotate(projected[:, :width].reshape(row_count, head_count, 64), cosine_part, sine_part)
            .astype(jnp.bfloat16)
            .reshape(row_count, width)
        )
        keys = (
            rotate(
                projected[:, width : 2 * width].reshape(row_count, head_count, 64),
                cosine_part,
                sine_part,
            )
            .astype(jnp.bfloat16)
            .reshape(row_count, width)
        )
        values = projected[:, 2 * width :].astype(jnp.bfloat16)
        query_groups = to_groups(queries)
        key_mine = to_groups(keys)
        value_mine = to_groups(values)
        key_all = jnp.concatenate([key_mine, seq_swap(key_mine, n_seq)], axis=1)
        value_all = jnp.concatenate([value_mine, seq_swap(value_mine, n_seq)], axis=1)
        mixed, row_max, row_total = lax.map(attend, (query_groups, key_all, value_all))
        attended = from_groups(mixed).astype(jnp.bfloat16)
        residual_mid = residual_in + (
            jnp.dot(attended, g_out, preferred_element_type=jnp.float32) + g_out_bias.astype(jnp.float32)
        )
        mid_gain = g_mid_gain.astype(jnp.float32)
        mid_shift = g_mid_shift.astype(jnp.float32)
        normed_mid = norm_rows(residual_mid, mid_gain, mid_shift).astype(jnp.bfloat16)
        upper = jnp.dot(normed_mid, g_expand, preferred_element_type=jnp.float32) + g_expand_bias.astype(
            jnp.float32
        )
        hidden = exact_gelu(upper).astype(jnp.bfloat16)
        result = residual_mid + (
            jnp.dot(hidden, g_reduce, preferred_element_type=jnp.float32) + g_reduce_bias.astype(jnp.float32)
        )
        block_output = result.astype(jnp.bfloat16)[None]

        grad_low = cotangent[0]
        grad_out = grad_low.astype(jnp.float32)
        reduce_term = jnp.einsum("tf,td->fd", hidden, grad_low, preferred_element_type=jnp.float32)
        reduce_offset_term = jnp.sum(grad_out, axis=0)
        chain_reduce = stage_one(reduce_term)
        grad_hidden = jnp.einsum("td,fd->tf", grad_low, g_reduce, preferred_element_type=jnp.float32)
        gelu_pull = jax.vjp(exact_gelu, upper)[1]
        grad_upper = gelu_pull(grad_hidden)[0].astype(jnp.bfloat16)
        expand_term = jnp.einsum("td,tf->df", normed_mid, grad_upper, preferred_element_type=jnp.float32)
        expand_offset_term = jnp.sum(grad_upper.astype(jnp.float32), axis=0)
        chain_expand = stage_one(expand_term)
        grad_mid_norm = jnp.einsum("tf,df->td", grad_upper, g_expand, preferred_element_type=jnp.float32)
        middle_pull = jax.vjp(norm_rows, residual_mid, mid_gain, mid_shift)[1]
        grad_mid_in, middle_gain_term, middle_shift_term = middle_pull(grad_mid_norm)
        grad_resid = grad_out + grad_mid_in
        grad_branch = grad_resid.astype(jnp.bfloat16)
        output_term = jnp.einsum("td,te->de", attended, grad_branch, preferred_element_type=jnp.float32)
        output_offset_term = jnp.sum(grad_branch.astype(jnp.float32), axis=0)
        chain_out = stage_one(output_term)
        grad_attended = jnp.einsum(
            "te,de->td", grad_branch, g_out, preferred_element_type=jnp.float32
        ).astype(jnp.bfloat16)
        chain_reduce, grad_attended = lax.optimization_barrier((chain_reduce, grad_attended))
        chain_reduce = stage_two(chain_reduce)
        query_grad, key_grad, value_grad = lax.map(
            attend_back,
            (query_groups, key_all, value_all, to_groups(grad_attended), row_max, row_total),
        )
        (chain_reduce, chain_expand, chain_out), (query_grad, key_grad, value_grad) = lax.optimization_barrier(
            ((chain_reduce, chain_expand, chain_out), (query_grad, key_grad, value_grad))
        )
        chain_reduce = stage_three(chain_reduce)
        chain_expand = stage_two(chain_expand)
        chain_out = stage_two(chain_out)
        half = row_count
        key_share = key_grad[:, :half] + seq_swap(
            key_grad[:, half:].astype(jnp.bfloat16), n_seq
        ).astype(jnp.float32)
        value_share = value_grad[:, :half] + seq_swap(
            value_grad[:, half:].astype(jnp.bfloat16), n_seq
        ).astype(jnp.float32)
        grad_query = rotate(
            from_groups(query_grad).reshape(row_count, head_count, 64), cosine_part, -sine_part
        ).reshape(row_count, width)
        grad_key = rotate(
            from_groups(key_share).reshape(row_count, head_count, 64), cosine_part, -sine_part
        ).reshape(row_count, width)
        grad_value = from_groups(value_share)
        grad_projected = jnp.concatenate([grad_query, grad_key, grad_value], axis=1).astype(jnp.bfloat16)
        joint_term = jnp.einsum("td,te->de", normed_in, grad_projected, preferred_element_type=jnp.float32)
        joint_offset_term = jnp.sum(grad_projected.astype(jnp.float32), axis=0)
        (chain_reduce, chain_expand, chain_out), grad_projected = lax.optimization_barrier(
            ((chain_reduce, chain_expand, chain_out), grad_projected)
        )
        chain_expand = stage_three(chain_expand)
        chain_out = stage_three(chain_out)
        chain_joint = stage_one(joint_term)
        grad_in_norm = jnp.einsum("te,de->td", grad_projected, g_joint, preferred_element_type=jnp.float32)
        input_pull = jax.vjp(norm_rows, residual_in, in_gain, in_shift)[1]
        grad_first_in, input_gain_term, input_shift_term = input_pull(grad_in_norm)
        input_gradient = (grad_resid + grad_first_in)[None]
        d_joint = stage_three(stage_two(chain_joint))
        d_reduce, d_expand, d_out = chain_reduce, chain_expand, chain_out
        (
            d_in_gain,
            d_in_shift,
            d_joint_bias,
            d_out_bias,
            d_mid_gain,
            d_mid_shift,
            d_expand_bias,
            d_reduce_bias,
        ) = reduce_vectors(
            [
                input_gain_term,
                input_shift_term,
                joint_offset_term,
                output_offset_term,
                middle_gain_term,
                middle_shift_term,
                expand_offset_term,
                reduce_offset_term,
            ]
        )
        return (
            block_output,
            input_gradient,
            d_in_gain,
            d_in_shift,
            d_joint,
            d_joint_bias,
            d_out,
            d_out_bias,
            d_mid_gain,
            d_mid_shift,
            d_expand,
            d_expand_bias,
            d_reduce,
            d_reduce_bias,
        )

    return local


def solution(mesh):
    return jax.shard_map(
        make_local(mesh),
        mesh=mesh,
        in_specs=(
            P(("rep", "fsdp"), "seq", None),
            P(None, ("rep", "fsdp"), "seq"),
            P("fsdp"),
            P("fsdp"),
            P("fsdp", None),
            P("fsdp"),
            P("fsdp", None),
            P("fsdp"),
            P("fsdp"),
            P("fsdp"),
            P("fsdp", None),
            P("fsdp"),
            P("fsdp", None),
            P("fsdp"),
            P(("rep", "fsdp"), "seq", None),
        ),
        out_specs=(
            P(("rep", "fsdp"), "seq", None),
            P(("rep", "fsdp"), "seq", None),
            P("fsdp"),
            P("fsdp"),
            P("fsdp", None),
            P("fsdp"),
            P("fsdp", None),
            P("fsdp"),
            P("fsdp"),
            P("fsdp"),
            P("fsdp", None),
            P("fsdp"),
            P("fsdp", None),
            P("fsdp"),
        ),
        check_vma=False,
    )
```

```python
import jax
import jax.numpy as jnp
from jax import lax
from jax.sharding import PartitionSpec as P

epsilon = 1e-06
LEVEL = ("rep", "seq")
LANES = 128


def norm_rows(values, gains, shifts):
    average = jnp.mean(values, axis=-1, keepdims=True)
    centred = values - average
    spread = jnp.mean(centred * centred, axis=-1, keepdims=True)
    return centred * lax.rsqrt(spread + epsilon) * gains + shifts


def rotary_tables(positions):
    counter = jnp.arange(10).astype(jnp.float32)
    frequency = jnp.power(10000.0, -counter / 10.0)
    angles = positions.astype(jnp.float32)[:, :, None] * frequency
    angles = jnp.transpose(angles, (1, 0, 2))
    return (jnp.cos(angles), jnp.sin(angles))


def rotate(values, cosine_part, sine_part):
    length = values.shape[0]
    heads_count = values.shape[1]
    turned = values[:, :, :60].reshape(length, heads_count, 3, 2, 10)
    former = turned[:, :, :, 0, :]
    latter = turned[:, :, :, 1, :]
    cosine_wide = cosine_part[:, None, :, :]
    sine_wide = sine_part[:, None, :, :]
    new_former = former * cosine_wide - latter * sine_wide
    new_latter = latter * cosine_wide + former * sine_wide
    joined = jnp.stack([new_former, new_latter], axis=3).reshape(length, heads_count, 60)
    return jnp.concatenate([joined, values[:, :, 60:]], axis=2)


def exact_gelu(values):
    return jax.nn.gelu(values, approximate=False)


def split_heads(block):
    return block.reshape(block.shape[0], block.shape[1] // 64, 64)


def group_scores(query_heads, key_heads):
    return (
        jnp.einsum("thd,shd->hts", query_heads, key_heads, preferred_element_type=jnp.float32)
        * 0.125
    )


def attend(inputs):
    query_block, key_block, value_block = inputs
    query_heads = split_heads(query_block)
    key_heads = split_heads(key_block)
    value_heads = split_heads(value_block)
    scores = group_scores(query_heads, key_heads)
    row_max = jnp.max(scores, axis=2, keepdims=True)
    raised = jnp.exp(scores - row_max)
    row_total = jnp.sum(raised, axis=2, keepdims=True)
    probs_low = (raised / row_total).astype(jnp.bfloat16)
    mixed = jnp.einsum("hts,shd->thd", probs_low, value_heads, preferred_element_type=jnp.float32)
    return (mixed.reshape(query_block.shape[0], -1), row_max, row_total)


def attend_back(inputs):
    query_block, key_block, value_block, grad_block, row_max, row_total = inputs
    query_heads = split_heads(query_block)
    key_heads = split_heads(key_block)
    value_heads = split_heads(value_block)
    grad_heads = split_heads(grad_block)
    scores = group_scores(query_heads, key_heads)
    probs = jnp.exp(scores - row_max) / row_total
    probs_low = probs.astype(jnp.bfloat16)
    grad_probs = jnp.einsum(
        "thd,shd->hts", grad_heads, value_heads, preferred_element_type=jnp.float32
    )
    value_grad = jnp.einsum(
        "hts,thd->shd", probs_low, grad_heads, preferred_element_type=jnp.float32
    )
    inner = jnp.sum(grad_probs * probs, axis=2, keepdims=True)
    grad_scores = (probs * (grad_probs - inner)).astype(jnp.bfloat16)
    query_grad = (
        jnp.einsum("hts,shd->thd", grad_scores, key_heads, preferred_element_type=jnp.float32)
        * 0.125
    )
    key_grad = (
        jnp.einsum("hts,thd->shd", grad_scores, query_heads, preferred_element_type=jnp.float32)
        * 0.125
    )
    return (
        query_grad.reshape(query_block.shape[0], -1),
        key_grad.reshape(key_block.shape[0], -1),
        value_grad.reshape(key_block.shape[0], -1),
    )


def make_comm(mesh):
    n_rep, n_fsdp, n_seq = mesh.shape["rep"], mesh.shape["fsdp"], mesh.shape["seq"]
    level = n_rep * n_seq
    bits = level.bit_length() - 1
    assert 1 << bits == level and n_seq & (n_seq - 1) == 0 and n_rep % 2 == 0
    assert n_fsdp & (n_fsdp - 1) == 0
    x_bits = list(range(n_seq.bit_length() - 1))
    core_bit = len(x_bits)
    y_bits = list(range(core_bit + 1, bits))

    def level_index():
        return lax.axis_index("rep") * n_seq + lax.axis_index("seq")

    def flip(bit):
        return [(k, k ^ (1 << bit)) for k in range(level)]

    def gather(piece, lead):
        k = level_index()
        blocks = [(piece, 0)]
        for bit in x_bits + y_bits + [core_bit]:
            blocks = blocks + [
                (lax.ppermute(block, LEVEL, flip(bit)), mask ^ (1 << bit)) for block, mask in blocks
            ]
        out = jnp.zeros((lead, level) + piece.shape[1:], piece.dtype)
        for block, mask in blocks:
            out = lax.dynamic_update_slice_in_dim(out, block[:, None], k ^ mask, axis=1)
        return out

    def reduce(total):
        k = level_index()
        lead = total.shape[0]
        acc = total.reshape((lead,) + (2,) * bits + total.shape[2:])
        alive = list(range(bits - 1, -1, -1))
        for bit in [core_bit] + y_bits[::-1] + x_bits[::-1]:
            axis = 1 + alive.index(bit)
            mine = (k >> bit) & 1
            keep = lax.dynamic_index_in_dim(acc, mine, axis, keepdims=False)
            send = lax.dynamic_index_in_dim(acc, 1 - mine, axis, keepdims=False)
            recv = lax.ppermute(send.astype(jnp.bfloat16), LEVEL, flip(bit))
            acc = keep.astype(jnp.float32) + recv.astype(jnp.float32)
            alive.remove(bit)
        return acc

    def line_reduce(acc):
        i = lax.axis_index("fsdp")
        n = n_fsdp
        up = [(a, a + 1) for a in range(n - 1)]
        down = [(a, a - 1) for a in range(1, n)]
        from_below = jnp.zeros(acc.shape[1:], jnp.float32)
        from_above = jnp.zeros(acc.shape[1:], jnp.float32)
        for step in range(1, n):
            j_up = jnp.clip(i + n - step, 0, n - 1)
            j_down = jnp.clip(i - (n - step), 0, n - 1)
            send_up = lax.dynamic_index_in_dim(acc, j_up, 0, keepdims=False) + from_below
            send_down = lax.dynamic_index_in_dim(acc, j_down, 0, keepdims=False) + from_above
            from_below = lax.ppermute(send_up.astype(jnp.bfloat16), "fsdp", up).astype(jnp.float32)
            from_above = lax.ppermute(send_down.astype(jnp.bfloat16), "fsdp", down).astype(jnp.float32)
        return lax.dynamic_index_in_dim(acc, i, 0, keepdims=False) + from_below + from_above

    def gather_weight(shard):
        rows, cols = shard.shape
        pieces = shard.reshape(level, rows // level, cols)
        mine = lax.dynamic_index_in_dim(pieces, level_index(), 0, keepdims=False)
        along = lax.all_gather(mine, "fsdp", axis=0, tiled=False)
        return gather(along, n_fsdp).reshape(n_fsdp * rows, cols)

    def reduce_weight(term):
        rows, cols = term.shape
        per = rows // (n_fsdp * level)
        acc = reduce(term.astype(jnp.bfloat16).reshape(n_fsdp, level, per, cols))
        share = line_reduce(acc).astype(jnp.bfloat16)
        return gather(share[None], 1).reshape(rows // n_fsdp, cols).astype(jnp.float32)

    def gather_vectors(shards):
        packed = jnp.concatenate(shards)
        full = lax.all_gather(packed, "fsdp", axis=0, tiled=False)
        outs = []
        at = 0
        for s in shards:
            outs.append(full[:, at : at + s.shape[0]].reshape(-1))
            at += s.shape[0]
        return outs

    def reduce_vectors(terms):
        total = jnp.concatenate(terms)
        for bit in range(bits):
            total = total + lax.ppermute(total, LEVEL, flip(bit))
        for bit in range(n_fsdp.bit_length() - 1):
            total = total + lax.ppermute(
                total, "fsdp", [(a, a ^ (1 << bit)) for a in range(n_fsdp)]
            )
        f = lax.axis_index("fsdp")
        outs = []
        at = 0
        for t in terms:
            own = t.shape[0] // n_fsdp
            outs.append(lax.dynamic_slice_in_dim(total, at + f * own, own))
            at += t.shape[0]
        return outs

    def gather_params(shards):
        return [gather_weight(s) if s.ndim == 2 else s for s in shards]

    def reduce_params(terms):
        return [reduce_weight(t) if t.ndim == 2 else t for t in terms]

    return gather_params, reduce_params, gather_vectors, reduce_vectors


def seq_swap(block, n_seq):
    if n_seq == 2:
        return lax.ppermute(block, "seq", [(0, 1), (1, 0)])
    raise NotImplementedError


def make_local(mesh):
    gather_params, reduce_params, gather_vectors, reduce_vectors = make_comm(mesh)
    n_seq = mesh.shape["seq"]

    def local(
        tokens,
        positions,
        input_gain,
        input_shift,
        joint_weight,
        joint_bias,
        output_weight,
        output_bias,
        middle_gain,
        middle_shift,
        expand_weight,
        expand_bias,
        reduce_weight,
        reduce_bias,
        cotangent,
    ):
        (
            g_in_gain,
            g_in_shift,
            g_joint_bias,
            g_out_bias,
            g_mid_gain,
            g_mid_shift,
            g_expand_bias,
            g_reduce_bias,
        ) = gather_vectors(
            [
                input_gain,
                input_shift,
                joint_bias,
                output_bias,
                middle_gain,
                middle_shift,
                expand_bias,
                reduce_bias,
            ]
        )
        g_joint, g_out, g_expand, g_reduce = gather_params(
            [joint_weight, output_weight, expand_weight, reduce_weight]
        )

        row_count = tokens.shape[1]
        width = tokens.shape[2]
        head_count = width // 64
        per_group = min(4, head_count)
        group_count = head_count // per_group
        group_width = per_group * 64

        def to_groups(block):
            return jnp.transpose(block.reshape(block.shape[0], group_count, group_width), (1, 0, 2))

        def from_groups(block):
            return jnp.transpose(block, (1, 0, 2)).reshape(block.shape[1], width)

        residual_in = tokens[0].astype(jnp.float32)
        cosine_part, sine_part = rotary_tables(positions[:, 0, :])
        in_gain = g_in_gain.astype(jnp.float32)
        in_shift = g_in_shift.astype(jnp.float32)
        normed_in = norm_rows(residual_in, in_gain, in_shift).astype(jnp.bfloat16)
        projected = jnp.dot(normed_in, g_joint, preferred_element_type=jnp.float32) + g_joint_bias.astype(
            jnp.float32
        )
        queries = (
            rotate(projected[:, :width].reshape(row_count, head_count, 64), cosine_part, sine_part)
            .astype(jnp.bfloat16)
            .reshape(row_count, width)
        )
        keys = (
            rotate(
                projected[:, width : 2 * width].reshape(row_count, head_count, 64),
                cosine_part,
                sine_part,
            )
            .astype(jnp.bfloat16)
            .reshape(row_count, width)
        )
        values = projected[:, 2 * width :].astype(jnp.bfloat16)
        query_groups = to_groups(queries)
        key_mine = to_groups(keys)
        value_mine = to_groups(values)
        key_all = jnp.concatenate([key_mine, seq_swap(key_mine, n_seq)], axis=1)
        value_all = jnp.concatenate([value_mine, seq_swap(value_mine, n_seq)], axis=1)
        mixed, row_max, row_total = lax.map(attend, (query_groups, key_all, value_all))
        attended = from_groups(mixed).astype(jnp.bfloat16)
        residual_mid = residual_in + (
            jnp.dot(attended, g_out, preferred_element_type=jnp.float32) + g_out_bias.astype(jnp.float32)
        )
        mid_gain = g_mid_gain.astype(jnp.float32)
        mid_shift = g_mid_shift.astype(jnp.float32)
        normed_mid = norm_rows(residual_mid, mid_gain, mid_shift).astype(jnp.bfloat16)
        upper = jnp.dot(normed_mid, g_expand, preferred_element_type=jnp.float32) + g_expand_bias.astype(
            jnp.float32
        )
        hidden = exact_gelu(upper).astype(jnp.bfloat16)
        result = residual_mid + (
            jnp.dot(hidden, g_reduce, preferred_element_type=jnp.float32) + g_reduce_bias.astype(jnp.float32)
        )
        block_output = result.astype(jnp.bfloat16)[None]

        grad_low = cotangent[0]
        grad_out = grad_low.astype(jnp.float32)
        reduce_term = jnp.einsum("tf,td->fd", hidden, grad_low, preferred_element_type=jnp.float32)
        reduce_offset_term = jnp.sum(grad_out, axis=0)
        (d_reduce,) = reduce_params([reduce_term])
        grad_hidden = jnp.einsum("td,fd->tf", grad_low, g_reduce, preferred_element_type=jnp.float32)
        gelu_pull = jax.vjp(exact_gelu, upper)[1]
        grad_upper = gelu_pull(grad_hidden)[0].astype(jnp.bfloat16)
        expand_term = jnp.einsum("td,tf->df", normed_mid, grad_upper, preferred_element_type=jnp.float32)
        expand_offset_term = jnp.sum(grad_upper.astype(jnp.float32), axis=0)
        (d_expand,) = reduce_params([expand_term])
        grad_mid_norm = jnp.einsum("tf,df->td", grad_upper, g_expand, preferred_element_type=jnp.float32)
        middle_pull = jax.vjp(norm_rows, residual_mid, mid_gain, mid_shift)[1]
        grad_mid_in, middle_gain_term, middle_shift_term = middle_pull(grad_mid_norm)
        grad_resid = grad_out + grad_mid_in
        grad_branch = grad_resid.astype(jnp.bfloat16)
        output_term = jnp.einsum("td,te->de", attended, grad_branch, preferred_element_type=jnp.float32)
        output_offset_term = jnp.sum(grad_branch.astype(jnp.float32), axis=0)
        (d_out,) = reduce_params([output_term])
        grad_attended = jnp.einsum(
            "te,de->td", grad_branch, g_out, preferred_element_type=jnp.float32
        ).astype(jnp.bfloat16)
        query_grad, key_grad, value_grad = lax.map(
            attend_back,
            (query_groups, key_all, value_all, to_groups(grad_attended), row_max, row_total),
        )
        half = row_count
        key_share = key_grad[:, :half] + seq_swap(
            key_grad[:, half:].astype(jnp.bfloat16), n_seq
        ).astype(jnp.float32)
        value_share = value_grad[:, :half] + seq_swap(
            value_grad[:, half:].astype(jnp.bfloat16), n_seq
        ).astype(jnp.float32)
        grad_query = rotate(
            from_groups(query_grad).reshape(row_count, head_count, 64), cosine_part, -sine_part
        ).reshape(row_count, width)
        grad_key = rotate(
            from_groups(key_share).reshape(row_count, head_count, 64), cosine_part, -sine_part
        ).reshape(row_count, width)
        grad_value = from_groups(value_share)
        grad_projected = jnp.concatenate([grad_query, grad_key, grad_value], axis=1).astype(jnp.bfloat16)
        joint_term = jnp.einsum("td,te->de", normed_in, grad_projected, preferred_element_type=jnp.float32)
        joint_offset_term = jnp.sum(grad_projected.astype(jnp.float32), axis=0)
        grad_in_norm = jnp.einsum("te,de->td", grad_projected, g_joint, preferred_element_type=jnp.float32)
        input_pull = jax.vjp(norm_rows, residual_in, in_gain, in_shift)[1]
        grad_first_in, input_gain_term, input_shift_term = input_pull(grad_in_norm)
        input_gradient = (grad_resid + grad_first_in)[None]
        (d_joint,) = reduce_params([joint_term])
        (
            d_in_gain,
            d_in_shift,
            d_joint_bias,
            d_out_bias,
            d_mid_gain,
            d_mid_shift,
            d_expand_bias,
            d_reduce_bias,
        ) = reduce_vectors(
            [
                input_gain_term,
                input_shift_term,
                joint_offset_term,
                output_offset_term,
                middle_gain_term,
                middle_shift_term,
                expand_offset_term,
                reduce_offset_term,
            ]
        )
        return (
            block_output,
            input_gradient,
            d_in_gain,
            d_in_shift,
            d_joint,
            d_joint_bias,
            d_out,
            d_out_bias,
            d_mid_gain,
            d_mid_shift,
            d_expand,
            d_expand_bias,
            d_reduce,
            d_reduce_bias,
        )

    return local


def solution(mesh):
    return jax.shard_map(
        make_local(mesh),
        mesh=mesh,
        in_specs=(
            P(("rep", "fsdp"), "seq", None),
            P(None, ("rep", "fsdp"), "seq"),
            P("fsdp"),
            P("fsdp"),
            P("fsdp", None),
            P("fsdp"),
            P("fsdp", None),
            P("fsdp"),
            P("fsdp"),
            P("fsdp"),
            P("fsdp", None),
            P("fsdp"),
            P("fsdp", None),
            P("fsdp"),
            P(("rep", "fsdp"), "seq", None),
        ),
        out_specs=(
            P(("rep", "fsdp"), "seq", None),
            P(("rep", "fsdp"), "seq", None),
            P("fsdp"),
            P("fsdp"),
            P("fsdp", None),
            P("fsdp"),
            P("fsdp", None),
            P("fsdp"),
            P("fsdp"),
            P("fsdp"),
            P("fsdp", None),
            P("fsdp"),
            P("fsdp", None),
            P("fsdp"),
        ),
        check_vma=False,
    )
```

```python
import jax
import jax.numpy as jnp
from jax import lax
from jax.sharding import PartitionSpec as P

epsilon = 1e-06
LEVEL = ("rep", "seq")
LANES = 128


def norm_rows(values, gains, shifts):
    average = jnp.mean(values, axis=-1, keepdims=True)
    centred = values - average
    spread = jnp.mean(centred * centred, axis=-1, keepdims=True)
    return centred * lax.rsqrt(spread + epsilon) * gains + shifts


def rotary_tables(positions):
    counter = jnp.arange(10).astype(jnp.float32)
    frequency = jnp.power(10000.0, -counter / 10.0)
    angles = positions.astype(jnp.float32)[:, :, None] * frequency
    angles = jnp.transpose(angles, (1, 0, 2))
    return (jnp.cos(angles), jnp.sin(angles))


def rotate(values, cosine_part, sine_part):
    length = values.shape[0]
    heads_count = values.shape[1]
    turned = values[:, :, :60].reshape(length, heads_count, 3, 2, 10)
    former = turned[:, :, :, 0, :]
    latter = turned[:, :, :, 1, :]
    cosine_wide = cosine_part[:, None, :, :]
    sine_wide = sine_part[:, None, :, :]
    new_former = former * cosine_wide - latter * sine_wide
    new_latter = latter * cosine_wide + former * sine_wide
    joined = jnp.stack([new_former, new_latter], axis=3).reshape(length, heads_count, 60)
    return jnp.concatenate([joined, values[:, :, 60:]], axis=2)


def exact_gelu(values):
    return jax.nn.gelu(values, approximate=False)


def split_heads(block):
    return block.reshape(block.shape[0], block.shape[1] // 64, 64)


def group_scores(query_heads, key_heads):
    return (
        jnp.einsum("thd,shd->hts", query_heads, key_heads, preferred_element_type=jnp.float32)
        * 0.125
    )


def attend(inputs):
    query_block, key_block, value_block = inputs
    query_heads = split_heads(query_block)
    key_heads = split_heads(key_block)
    value_heads = split_heads(value_block)
    scores = group_scores(query_heads, key_heads)
    row_max = jnp.max(scores, axis=2, keepdims=True)
    raised = jnp.exp(scores - row_max)
    row_total = jnp.sum(raised, axis=2, keepdims=True)
    probs_low = (raised / row_total).astype(jnp.bfloat16)
    mixed = jnp.einsum("hts,shd->thd", probs_low, value_heads, preferred_element_type=jnp.float32)
    return (mixed.reshape(query_block.shape[0], -1), row_max, row_total)


def attend_back(inputs):
    query_block, key_block, value_block, grad_block, row_max, row_total = inputs
    query_heads = split_heads(query_block)
    key_heads = split_heads(key_block)
    value_heads = split_heads(value_block)
    grad_heads = split_heads(grad_block)
    scores = group_scores(query_heads, key_heads)
    probs = jnp.exp(scores - row_max) / row_total
    probs_low = probs.astype(jnp.bfloat16)
    grad_probs = jnp.einsum(
        "thd,shd->hts", grad_heads, value_heads, preferred_element_type=jnp.float32
    )
    value_grad = jnp.einsum(
        "hts,thd->shd", probs_low, grad_heads, preferred_element_type=jnp.float32
    )
    inner = jnp.sum(grad_probs * probs, axis=2, keepdims=True)
    grad_scores = (probs * (grad_probs - inner)).astype(jnp.bfloat16)
    query_grad = (
        jnp.einsum("hts,shd->thd", grad_scores, key_heads, preferred_element_type=jnp.float32)
        * 0.125
    )
    key_grad = (
        jnp.einsum("hts,thd->shd", grad_scores, query_heads, preferred_element_type=jnp.float32)
        * 0.125
    )
    return (
        query_grad.reshape(query_block.shape[0], -1),
        key_grad.reshape(key_block.shape[0], -1),
        value_grad.reshape(key_block.shape[0], -1),
    )


def make_comm(mesh):
    n_rep, n_fsdp, n_seq = mesh.shape["rep"], mesh.shape["fsdp"], mesh.shape["seq"]
    level = n_rep * n_seq
    bits = level.bit_length() - 1
    assert 1 << bits == level and n_seq & (n_seq - 1) == 0 and n_rep % 2 == 0
    assert n_fsdp & (n_fsdp - 1) == 0
    x_bits = list(range(n_seq.bit_length() - 1))
    core_bit = len(x_bits)
    y_bits = list(range(core_bit + 1, bits))

    def level_index():
        return lax.axis_index("rep") * n_seq + lax.axis_index("seq")

    def flip(bit):
        return [(k, k ^ (1 << bit)) for k in range(level)]

    def gather(piece, lead):
        k = level_index()
        blocks = [(piece, 0)]
        for bit in x_bits + y_bits + [core_bit]:
            blocks = blocks + [
                (lax.ppermute(block, LEVEL, flip(bit)), mask ^ (1 << bit)) for block, mask in blocks
            ]
        out = jnp.zeros((lead, level) + piece.shape[1:], piece.dtype)
        for block, mask in blocks:
            out = lax.dynamic_update_slice_in_dim(out, block[:, None], k ^ mask, axis=1)
        return out

    def reduce(total):
        k = level_index()
        lead = total.shape[0]
        acc = total.reshape((lead,) + (2,) * bits + total.shape[2:])
        alive = list(range(bits - 1, -1, -1))
        for bit in [core_bit] + y_bits[::-1] + x_bits[::-1]:
            axis = 1 + alive.index(bit)
            mine = (k >> bit) & 1
            keep = lax.dynamic_index_in_dim(acc, mine, axis, keepdims=False)
            send = lax.dynamic_index_in_dim(acc, 1 - mine, axis, keepdims=False)
            recv = lax.ppermute(send.astype(jnp.bfloat16), LEVEL, flip(bit))
            acc = keep.astype(jnp.float32) + recv.astype(jnp.float32)
            alive.remove(bit)
        return acc

    def line_reduce(acc):
        i = lax.axis_index("fsdp")
        n = n_fsdp
        up = [(a, a + 1) for a in range(n - 1)]
        down = [(a, a - 1) for a in range(1, n)]
        from_below = jnp.zeros(acc.shape[1:], jnp.float32)
        from_above = jnp.zeros(acc.shape[1:], jnp.float32)
        for step in range(1, n):
            j_up = jnp.clip(i + n - step, 0, n - 1)
            j_down = jnp.clip(i - (n - step), 0, n - 1)
            send_up = lax.dynamic_index_in_dim(acc, j_up, 0, keepdims=False) + from_below
            send_down = lax.dynamic_index_in_dim(acc, j_down, 0, keepdims=False) + from_above
            from_below = lax.ppermute(send_up.astype(jnp.bfloat16), "fsdp", up).astype(jnp.float32)
            from_above = lax.ppermute(send_down.astype(jnp.bfloat16), "fsdp", down).astype(jnp.float32)
        return lax.dynamic_index_in_dim(acc, i, 0, keepdims=False) + from_below + from_above

    def gather_weight(shard):
        rows, cols = shard.shape
        pieces = shard.reshape(level, rows // level, cols)
        mine = lax.dynamic_index_in_dim(pieces, level_index(), 0, keepdims=False)
        along = lax.all_gather(mine, "fsdp", axis=0, tiled=False)
        return gather(along, n_fsdp).reshape(n_fsdp * rows, cols)

    def reduce_weight(term):
        rows, cols = term.shape
        per = rows // (n_fsdp * level)
        acc = reduce(term.astype(jnp.bfloat16).reshape(n_fsdp, level, per, cols))
        share = line_reduce(acc).astype(jnp.bfloat16)
        return gather(share[None], 1).reshape(rows // n_fsdp, cols).astype(jnp.float32)

    def line_gather(piece):
        i = lax.axis_index("fsdp")
        n = n_fsdp
        up = [(a, a + 1) for a in range(n - 1)]
        down = [(a, a - 1) for a in range(1, n)]
        out = jnp.zeros((n + 1,) + piece.shape, piece.dtype)
        out = lax.dynamic_update_slice_in_dim(out, piece[None], i, axis=0)
        from_below = piece
        from_above = piece
        for step in range(1, n):
            from_below = lax.ppermute(from_below, "fsdp", up)
            from_above = lax.ppermute(from_above, "fsdp", down)
            below_at = jnp.where(i - step >= 0, i - step, n)
            above_at = jnp.where(i + step < n, i + step, n)
            out = lax.dynamic_update_slice_in_dim(out, from_below[None], below_at, axis=0)
            out = lax.dynamic_update_slice_in_dim(out, from_above[None], above_at, axis=0)
        return out[:n]

    def gather_first(shard, vectors):
        rows, cols = shard.shape
        per = rows // level
        mine = lax.dynamic_index_in_dim(shard.reshape(level, per, cols), level_index(), 0, keepdims=False)
        lengths = [v.shape[0] for v in vectors]
        weight_rows = per * cols // LANES
        vector_rows = -(-sum(lengths) // LANES)
        total_rows = -(-(weight_rows + vector_rows) // 16) * 16
        flat_vec = jnp.pad(jnp.concatenate(vectors), (0, total_rows * LANES - weight_rows * LANES - sum(lengths)))
        packed = jnp.concatenate([mine.reshape(weight_rows, LANES), flat_vec.reshape(-1, LANES)], axis=0)
        along = line_gather(packed)
        weight_part = along[:, :weight_rows].reshape(n_fsdp, per, cols)
        full = gather(weight_part, n_fsdp).reshape(n_fsdp * rows, cols)
        vec_part = along[:, weight_rows:].reshape(n_fsdp, -1)
        outs = []
        at = 0
        for length in lengths:
            outs.append(vec_part[:, at : at + length].reshape(-1))
            at += length
        return full, outs

    def gather_vectors(shards):
        packed = jnp.concatenate(shards)
        full = lax.all_gather(packed, "fsdp", axis=0, tiled=False)
        outs = []
        at = 0
        for s in shards:
            outs.append(full[:, at : at + s.shape[0]].reshape(-1))
            at += s.shape[0]
        return outs

    def reduce_vectors(terms):
        total = jnp.concatenate(terms)
        for bit in range(bits):
            total = total + lax.ppermute(total, LEVEL, flip(bit))
        for bit in range(n_fsdp.bit_length() - 1):
            total = total + lax.ppermute(
                total, "fsdp", [(a, a ^ (1 << bit)) for a in range(n_fsdp)]
            )
        f = lax.axis_index("fsdp")
        outs = []
        at = 0
        for t in terms:
            own = t.shape[0] // n_fsdp
            outs.append(lax.dynamic_slice_in_dim(total, at + f * own, own))
            at += t.shape[0]
        return outs

    def gather_params(shards):
        return [gather_weight(s) if s.ndim == 2 else s for s in shards]

    def reduce_params(terms):
        return [reduce_weight(t) if t.ndim == 2 else t for t in terms]

    return gather_params, reduce_params, gather_first, reduce_vectors


def seq_swap(block, n_seq):
    if n_seq == 2:
        return lax.ppermute(block, "seq", [(0, 1), (1, 0)])
    raise NotImplementedError


def make_local(mesh):
    gather_params, reduce_params, gather_first, reduce_vectors = make_comm(mesh)
    n_seq = mesh.shape["seq"]

    def local(
        tokens,
        positions,
        input_gain,
        input_shift,
        joint_weight,
        joint_bias,
        output_weight,
        output_bias,
        middle_gain,
        middle_shift,
        expand_weight,
        expand_bias,
        reduce_weight,
        reduce_bias,
        cotangent,
    ):
        g_joint, (
            g_in_gain,
            g_in_shift,
            g_joint_bias,
            g_out_bias,
            g_mid_gain,
            g_mid_shift,
            g_expand_bias,
            g_reduce_bias,
        ) = gather_first(
            joint_weight,
            [
                input_gain,
                input_shift,
                joint_bias,
                output_bias,
                middle_gain,
                middle_shift,
                expand_bias,
                reduce_bias,
            ],
        )
        g_out, g_expand, g_reduce = gather_params([output_weight, expand_weight, reduce_weight])

        row_count = tokens.shape[1]
        width = tokens.shape[2]
        head_count = width // 64
        per_group = min(4, head_count)
        group_count = head_count // per_group
        group_width = per_group * 64

        def to_groups(block):
            return jnp.transpose(block.reshape(block.shape[0], group_count, group_width), (1, 0, 2))

        def from_groups(block):
            return jnp.transpose(block, (1, 0, 2)).reshape(block.shape[1], width)

        residual_in = tokens[0].astype(jnp.float32)
        cosine_part, sine_part = rotary_tables(positions[:, 0, :])
        in_gain = g_in_gain.astype(jnp.float32)
        in_shift = g_in_shift.astype(jnp.float32)
        normed_in = norm_rows(residual_in, in_gain, in_shift).astype(jnp.bfloat16)
        projected = jnp.dot(normed_in, g_joint, preferred_element_type=jnp.float32) + g_joint_bias.astype(
            jnp.float32
        )
        queries = (
            rotate(projected[:, :width].reshape(row_count, head_count, 64), cosine_part, sine_part)
            .astype(jnp.bfloat16)
            .reshape(row_count, width)
        )
        keys = (
            rotate(
                projected[:, width : 2 * width].reshape(row_count, head_count, 64),
                cosine_part,
                sine_part,
            )
            .astype(jnp.bfloat16)
            .reshape(row_count, width)
        )
        values = projected[:, 2 * width :].astype(jnp.bfloat16)
        query_groups = to_groups(queries)
        key_mine = to_groups(keys)
        value_mine = to_groups(values)
        key_all = jnp.concatenate([key_mine, seq_swap(key_mine, n_seq)], axis=1)
        value_all = jnp.concatenate([value_mine, seq_swap(value_mine, n_seq)], axis=1)
        mixed, row_max, row_total = lax.map(attend, (query_groups, key_all, value_all))
        attended = from_groups(mixed).astype(jnp.bfloat16)
        residual_mid = residual_in + (
            jnp.dot(attended, g_out, preferred_element_type=jnp.float32) + g_out_bias.astype(jnp.float32)
        )
        mid_gain = g_mid_gain.astype(jnp.float32)
        mid_shift = g_mid_shift.astype(jnp.float32)
        normed_mid = norm_rows(residual_mid, mid_gain, mid_shift).astype(jnp.bfloat16)
        upper = jnp.dot(normed_mid, g_expand, preferred_element_type=jnp.float32) + g_expand_bias.astype(
            jnp.float32
        )
        hidden = exact_gelu(upper).astype(jnp.bfloat16)
        result = residual_mid + (
            jnp.dot(hidden, g_reduce, preferred_element_type=jnp.float32) + g_reduce_bias.astype(jnp.float32)
        )
        block_output = result.astype(jnp.bfloat16)[None]

        grad_low = cotangent[0]
        grad_out = grad_low.astype(jnp.float32)
        reduce_term = jnp.einsum("tf,td->fd", hidden, grad_low, preferred_element_type=jnp.float32)
        reduce_offset_term = jnp.sum(grad_out, axis=0)
        (d_reduce,) = reduce_params([reduce_term])
        grad_hidden = jnp.einsum("td,fd->tf", grad_low, g_reduce, preferred_element_type=jnp.float32)
        gelu_pull = jax.vjp(exact_gelu, upper)[1]
        grad_upper = gelu_pull(grad_hidden)[0].astype(jnp.bfloat16)
        expand_term = jnp.einsum("td,tf->df", normed_mid, grad_upper, preferred_element_type=jnp.float32)
        expand_offset_term = jnp.sum(grad_upper.astype(jnp.float32), axis=0)
        (d_expand,) = reduce_params([expand_term])
        grad_mid_norm = jnp.einsum("tf,df->td", grad_upper, g_expand, preferred_element_type=jnp.float32)
        middle_pull = jax.vjp(norm_rows, residual_mid, mid_gain, mid_shift)[1]
        grad_mid_in, middle_gain_term, middle_shift_term = middle_pull(grad_mid_norm)
        grad_resid = grad_out + grad_mid_in
        grad_branch = grad_resid.astype(jnp.bfloat16)
        output_term = jnp.einsum("td,te->de", attended, grad_branch, preferred_element_type=jnp.float32)
        output_offset_term = jnp.sum(grad_branch.astype(jnp.float32), axis=0)
        (d_out,) = reduce_params([output_term])
        grad_attended = jnp.einsum(
            "te,de->td", grad_branch, g_out, preferred_element_type=jnp.float32
        ).astype(jnp.bfloat16)
        query_grad, key_grad, value_grad = lax.map(
            attend_back,
            (query_groups, key_all, value_all, to_groups(grad_attended), row_max, row_total),
        )
        half = row_count
        key_share = key_grad[:, :half] + seq_swap(
            key_grad[:, half:].astype(jnp.bfloat16), n_seq
        ).astype(jnp.float32)
        value_share = value_grad[:, :half] + seq_swap(
            value_grad[:, half:].astype(jnp.bfloat16), n_seq
        ).astype(jnp.float32)
        grad_query = rotate(
            from_groups(query_grad).reshape(row_count, head_count, 64), cosine_part, -sine_part
        ).reshape(row_count, width)
        grad_key = rotate(
            from_groups(key_share).reshape(row_count, head_count, 64), cosine_part, -sine_part
        ).reshape(row_count, width)
        grad_value = from_groups(value_share)
        grad_projected = jnp.concatenate([grad_query, grad_key, grad_value], axis=1).astype(jnp.bfloat16)
        joint_term = jnp.einsum("td,te->de", normed_in, grad_projected, preferred_element_type=jnp.float32)
        joint_offset_term = jnp.sum(grad_projected.astype(jnp.float32), axis=0)
        grad_in_norm = jnp.einsum("te,de->td", grad_projected, g_joint, preferred_element_type=jnp.float32)
        input_pull = jax.vjp(norm_rows, residual_in, in_gain, in_shift)[1]
        grad_first_in, input_gain_term, input_shift_term = input_pull(grad_in_norm)
        input_gradient = (grad_resid + grad_first_in)[None]
        (d_joint,) = reduce_params([joint_term])
        (
            d_in_gain,
            d_in_shift,
            d_joint_bias,
            d_out_bias,
            d_mid_gain,
            d_mid_shift,
            d_expand_bias,
            d_reduce_bias,
        ) = reduce_vectors(
            [
                input_gain_term,
                input_shift_term,
                joint_offset_term,
                output_offset_term,
                middle_gain_term,
                middle_shift_term,
                expand_offset_term,
                reduce_offset_term,
            ]
        )
        return (
            block_output,
            input_gradient,
            d_in_gain,
            d_in_shift,
            d_joint,
            d_joint_bias,
            d_out,
            d_out_bias,
            d_mid_gain,
            d_mid_shift,
            d_expand,
            d_expand_bias,
            d_reduce,
            d_reduce_bias,
        )

    return local


def solution(mesh):
    return jax.shard_map(
        make_local(mesh),
        mesh=mesh,
        in_specs=(
            P(("rep", "fsdp"), "seq", None),
            P(None, ("rep", "fsdp"), "seq"),
            P("fsdp"),
            P("fsdp"),
            P("fsdp", None),
            P("fsdp"),
            P("fsdp", None),
            P("fsdp"),
            P("fsdp"),
            P("fsdp"),
            P("fsdp", None),
            P("fsdp"),
            P("fsdp", None),
            P("fsdp"),
            P(("rep", "fsdp"), "seq", None),
        ),
        out_specs=(
            P(("rep", "fsdp"), "seq", None),
            P(("rep", "fsdp"), "seq", None),
            P("fsdp"),
            P("fsdp"),
            P("fsdp", None),
            P("fsdp"),
            P("fsdp", None),
            P("fsdp"),
            P("fsdp"),
            P("fsdp"),
            P("fsdp", None),
            P("fsdp"),
            P("fsdp", None),
            P("fsdp"),
        ),
        check_vma=False,
    )
```

```python
import jax
import jax.numpy as jnp
from jax import lax
from jax.sharding import PartitionSpec as P

epsilon = 1e-06
LEVEL = ("rep", "seq")
LANES = 128


def norm_rows(values, gains, shifts):
    average = jnp.mean(values, axis=-1, keepdims=True)
    centred = values - average
    spread = jnp.mean(centred * centred, axis=-1, keepdims=True)
    return centred * lax.rsqrt(spread + epsilon) * gains + shifts


def rotary_tables(positions):
    counter = jnp.arange(10).astype(jnp.float32)
    frequency = jnp.power(10000.0, -counter / 10.0)
    angles = positions.astype(jnp.float32)[:, :, None] * frequency
    angles = jnp.transpose(angles, (1, 0, 2))
    return (jnp.cos(angles), jnp.sin(angles))


def rotate(values, cosine_part, sine_part):
    length = values.shape[0]
    heads_count = values.shape[1]
    turned = values[:, :, :60].reshape(length, heads_count, 3, 2, 10)
    former = turned[:, :, :, 0, :]
    latter = turned[:, :, :, 1, :]
    cosine_wide = cosine_part[:, None, :, :]
    sine_wide = sine_part[:, None, :, :]
    new_former = former * cosine_wide - latter * sine_wide
    new_latter = latter * cosine_wide + former * sine_wide
    joined = jnp.stack([new_former, new_latter], axis=3).reshape(length, heads_count, 60)
    return jnp.concatenate([joined, values[:, :, 60:]], axis=2)


def exact_gelu(values):
    return jax.nn.gelu(values, approximate=False)


def split_heads(block):
    return block.reshape(block.shape[0], block.shape[1] // 64, 64)


def group_scores(query_heads, key_heads):
    return (
        jnp.einsum("thd,shd->hts", query_heads, key_heads, preferred_element_type=jnp.float32)
        * 0.125
    )


def attend(inputs):
    query_block, key_block, value_block = inputs
    query_heads = split_heads(query_block)
    key_heads = split_heads(key_block)
    value_heads = split_heads(value_block)
    scores = group_scores(query_heads, key_heads)
    row_max = jnp.max(scores, axis=2, keepdims=True)
    raised = jnp.exp(scores - row_max)
    row_total = jnp.sum(raised, axis=2, keepdims=True)
    probs_low = (raised / row_total).astype(jnp.bfloat16)
    mixed = jnp.einsum("hts,shd->thd", probs_low, value_heads, preferred_element_type=jnp.float32)
    return (mixed.reshape(query_block.shape[0], -1), row_max, row_total)


def attend_back(inputs):
    query_block, key_block, value_block, grad_block, row_max, row_total = inputs
    query_heads = split_heads(query_block)
    key_heads = split_heads(key_block)
    value_heads = split_heads(value_block)
    grad_heads = split_heads(grad_block)
    scores = group_scores(query_heads, key_heads)
    probs = jnp.exp(scores - row_max) / row_total
    probs_low = probs.astype(jnp.bfloat16)
    grad_probs = jnp.einsum(
        "thd,shd->hts", grad_heads, value_heads, preferred_element_type=jnp.float32
    )
    value_grad = jnp.einsum(
        "hts,thd->shd", probs_low, grad_heads, preferred_element_type=jnp.float32
    )
    inner = jnp.sum(grad_probs * probs, axis=2, keepdims=True)
    grad_scores = (probs * (grad_probs - inner)).astype(jnp.bfloat16)
    query_grad = (
        jnp.einsum("hts,shd->thd", grad_scores, key_heads, preferred_element_type=jnp.float32)
        * 0.125
    )
    key_grad = (
        jnp.einsum("hts,thd->shd", grad_scores, query_heads, preferred_element_type=jnp.float32)
        * 0.125
    )
    return (
        query_grad.reshape(query_block.shape[0], -1),
        key_grad.reshape(key_block.shape[0], -1),
        value_grad.reshape(key_block.shape[0], -1),
    )


def make_comm(mesh):
    n_rep, n_fsdp, n_seq = mesh.shape["rep"], mesh.shape["fsdp"], mesh.shape["seq"]
    level = n_rep * n_seq
    bits = level.bit_length() - 1
    assert 1 << bits == level and n_seq & (n_seq - 1) == 0 and n_rep % 2 == 0
    assert n_fsdp & (n_fsdp - 1) == 0
    x_bits = list(range(n_seq.bit_length() - 1))
    core_bit = len(x_bits)
    y_bits = list(range(core_bit + 1, bits))

    def level_index():
        return lax.axis_index("rep") * n_seq + lax.axis_index("seq")

    def flip(bit):
        return [(k, k ^ (1 << bit)) for k in range(level)]

    def gather(piece, lead, order=None):
        k = level_index()
        blocks = [(piece, 0)]
        for bit in order or (x_bits + y_bits + [core_bit]):
            blocks = blocks + [
                (lax.ppermute(block, LEVEL, flip(bit)), mask ^ (1 << bit)) for block, mask in blocks
            ]
        out = jnp.zeros((lead, level) + piece.shape[1:], piece.dtype)
        for block, mask in blocks:
            out = lax.dynamic_update_slice_in_dim(out, block[:, None], k ^ mask, axis=1)
        return out

    def reduce(total):
        k = level_index()
        lead = total.shape[0]
        acc = total.reshape((lead,) + (2,) * bits + total.shape[2:])
        alive = list(range(bits - 1, -1, -1))
        for bit in [core_bit] + y_bits[::-1] + x_bits[::-1]:
            axis = 1 + alive.index(bit)
            mine = (k >> bit) & 1
            keep = lax.dynamic_index_in_dim(acc, mine, axis, keepdims=False)
            send = lax.dynamic_index_in_dim(acc, 1 - mine, axis, keepdims=False)
            recv = lax.ppermute(send.astype(jnp.bfloat16), LEVEL, flip(bit))
            acc = keep.astype(jnp.float32) + recv.astype(jnp.float32)
            alive.remove(bit)
        return acc

    def line_reduce(acc):
        i = lax.axis_index("fsdp")
        n = n_fsdp
        up = [(a, a + 1) for a in range(n - 1)]
        down = [(a, a - 1) for a in range(1, n)]
        from_below = jnp.zeros(acc.shape[1:], jnp.float32)
        from_above = jnp.zeros(acc.shape[1:], jnp.float32)
        for step in range(1, n):
            j_up = jnp.clip(i + n - step, 0, n - 1)
            j_down = jnp.clip(i - (n - step), 0, n - 1)
            send_up = lax.dynamic_index_in_dim(acc, j_up, 0, keepdims=False) + from_below
            send_down = lax.dynamic_index_in_dim(acc, j_down, 0, keepdims=False) + from_above
            from_below = lax.ppermute(send_up.astype(jnp.bfloat16), "fsdp", up).astype(jnp.float32)
            from_above = lax.ppermute(send_down.astype(jnp.bfloat16), "fsdp", down).astype(jnp.float32)
        return lax.dynamic_index_in_dim(acc, i, 0, keepdims=False) + from_below + from_above

    def gather_weight(shard):
        rows, cols = shard.shape
        pieces = shard.reshape(level, rows // level, cols)
        mine = lax.dynamic_index_in_dim(pieces, level_index(), 0, keepdims=False)
        along = lax.all_gather(mine, "fsdp", axis=0, tiled=False)
        return gather(along, n_fsdp).reshape(n_fsdp * rows, cols)

    def reduce_weight(term):
        rows, cols = term.shape
        per = rows // (n_fsdp * level)
        acc = reduce(term.astype(jnp.bfloat16).reshape(n_fsdp, level, per, cols))
        share = line_reduce(acc).astype(jnp.bfloat16)
        full = gather(share[None], 1, y_bits + x_bits + [core_bit])
        return full.reshape(rows // n_fsdp, cols).astype(jnp.float32)

    def gather_vectors(shards):
        packed = jnp.concatenate(shards)
        full = lax.all_gather(packed, "fsdp", axis=0, tiled=False)
        outs = []
        at = 0
        for s in shards:
            outs.append(full[:, at : at + s.shape[0]].reshape(-1))
            at += s.shape[0]
        return outs

    def reduce_vectors(terms):
        total = jnp.concatenate(terms)
        for bit in range(bits):
            total = total + lax.ppermute(total, LEVEL, flip(bit))
        for bit in range(n_fsdp.bit_length() - 1):
            total = total + lax.ppermute(
                total, "fsdp", [(a, a ^ (1 << bit)) for a in range(n_fsdp)]
            )
        f = lax.axis_index("fsdp")
        outs = []
        at = 0
        for t in terms:
            own = t.shape[0] // n_fsdp
            outs.append(lax.dynamic_slice_in_dim(total, at + f * own, own))
            at += t.shape[0]
        return outs

    def gather_params(shards):
        return [gather_weight(s) if s.ndim == 2 else s for s in shards]

    def reduce_params(terms):
        return [reduce_weight(t) if t.ndim == 2 else t for t in terms]

    return gather_params, reduce_params, gather_vectors, reduce_vectors


def seq_swap(block, n_seq):
    if n_seq == 2:
        return lax.ppermute(block, "seq", [(0, 1), (1, 0)])
    raise NotImplementedError


def make_local(mesh):
    gather_params, reduce_params, gather_vectors, reduce_vectors = make_comm(mesh)
    n_seq = mesh.shape["seq"]

    def local(
        tokens,
        positions,
        input_gain,
        input_shift,
        joint_weight,
        joint_bias,
        output_weight,
        output_bias,
        middle_gain,
        middle_shift,
        expand_weight,
        expand_bias,
        reduce_weight,
        reduce_bias,
        cotangent,
    ):
        (
            g_in_gain,
            g_in_shift,
            g_joint_bias,
            g_out_bias,
            g_mid_gain,
            g_mid_shift,
            g_expand_bias,
            g_reduce_bias,
        ) = gather_vectors(
            [
                input_gain,
                input_shift,
                joint_bias,
                output_bias,
                middle_gain,
                middle_shift,
                expand_bias,
                reduce_bias,
            ]
        )
        g_joint, g_out, g_expand, g_reduce = gather_params(
            [joint_weight, output_weight, expand_weight, reduce_weight]
        )

        row_count = tokens.shape[1]
        width = tokens.shape[2]
        head_count = width // 64
        per_group = min(4, head_count)
        group_count = head_count // per_group
        group_width = per_group * 64

        def to_groups(block):
            return jnp.transpose(block.reshape(block.shape[0], group_count, group_width), (1, 0, 2))

        def from_groups(block):
            return jnp.transpose(block, (1, 0, 2)).reshape(block.shape[1], width)

        residual_in = tokens[0].astype(jnp.float32)
        cosine_part, sine_part = rotary_tables(positions[:, 0, :])
        in_gain = g_in_gain.astype(jnp.float32)
        in_shift = g_in_shift.astype(jnp.float32)
        normed_in = norm_rows(residual_in, in_gain, in_shift).astype(jnp.bfloat16)
        projected = jnp.dot(normed_in, g_joint, preferred_element_type=jnp.float32) + g_joint_bias.astype(
            jnp.float32
        )
        queries = (
            rotate(projected[:, :width].reshape(row_count, head_count, 64), cosine_part, sine_part)
            .astype(jnp.bfloat16)
            .reshape(row_count, width)
        )
        keys = (
            rotate(
                projected[:, width : 2 * width].reshape(row_count, head_count, 64),
                cosine_part,
                sine_part,
            )
            .astype(jnp.bfloat16)
            .reshape(row_count, width)
        )
        values = projected[:, 2 * width :].astype(jnp.bfloat16)
        query_groups = to_groups(queries)
        key_mine = to_groups(keys)
        value_mine = to_groups(values)
        key_all = jnp.concatenate([key_mine, seq_swap(key_mine, n_seq)], axis=1)
        value_all = jnp.concatenate([value_mine, seq_swap(value_mine, n_seq)], axis=1)
        mixed, row_max, row_total = lax.map(attend, (query_groups, key_all, value_all))
        attended = from_groups(mixed).astype(jnp.bfloat16)
        residual_mid = residual_in + (
            jnp.dot(attended, g_out, preferred_element_type=jnp.float32) + g_out_bias.astype(jnp.float32)
        )
        mid_gain = g_mid_gain.astype(jnp.float32)
        mid_shift = g_mid_shift.astype(jnp.float32)
        normed_mid = norm_rows(residual_mid, mid_gain, mid_shift).astype(jnp.bfloat16)
        upper = jnp.dot(normed_mid, g_expand, preferred_element_type=jnp.float32) + g_expand_bias.astype(
            jnp.float32
        )
        hidden = exact_gelu(upper).astype(jnp.bfloat16)
        result = residual_mid + (
            jnp.dot(hidden, g_reduce, preferred_element_type=jnp.float32) + g_reduce_bias.astype(jnp.float32)
        )
        block_output = result.astype(jnp.bfloat16)[None]

        grad_low = cotangent[0]
        grad_out = grad_low.astype(jnp.float32)
        reduce_term = jnp.einsum("tf,td->fd", hidden, grad_low, preferred_element_type=jnp.float32)
        reduce_offset_term = jnp.sum(grad_out, axis=0)
        (d_reduce,) = reduce_params([reduce_term])
        grad_hidden = jnp.einsum("td,fd->tf", grad_low, g_reduce, preferred_element_type=jnp.float32)
        gelu_pull = jax.vjp(exact_gelu, upper)[1]
        grad_upper = gelu_pull(grad_hidden)[0].astype(jnp.bfloat16)
        expand_term = jnp.einsum("td,tf->df", normed_mid, grad_upper, preferred_element_type=jnp.float32)
        expand_offset_term = jnp.sum(grad_upper.astype(jnp.float32), axis=0)
        (d_expand,) = reduce_params([expand_term])
        grad_mid_norm = jnp.einsum("tf,df->td", grad_upper, g_expand, preferred_element_type=jnp.float32)
        middle_pull = jax.vjp(norm_rows, residual_mid, mid_gain, mid_shift)[1]
        grad_mid_in, middle_gain_term, middle_shift_term = middle_pull(grad_mid_norm)
        grad_resid = grad_out + grad_mid_in
        grad_branch = grad_resid.astype(jnp.bfloat16)
        output_term = jnp.einsum("td,te->de", attended, grad_branch, preferred_element_type=jnp.float32)
        output_offset_term = jnp.sum(grad_branch.astype(jnp.float32), axis=0)
        (d_out,) = reduce_params([output_term])
        grad_attended = jnp.einsum(
            "te,de->td", grad_branch, g_out, preferred_element_type=jnp.float32
        ).astype(jnp.bfloat16)
        query_grad, key_grad, value_grad = lax.map(
            attend_back,
            (query_groups, key_all, value_all, to_groups(grad_attended), row_max, row_total),
        )
        half = row_count
        key_share = key_grad[:, :half] + seq_swap(
            key_grad[:, half:].astype(jnp.bfloat16), n_seq
        ).astype(jnp.float32)
        value_share = value_grad[:, :half] + seq_swap(
            value_grad[:, half:].astype(jnp.bfloat16), n_seq
        ).astype(jnp.float32)
        grad_query = rotate(
            from_groups(query_grad).reshape(row_count, head_count, 64), cosine_part, -sine_part
        ).reshape(row_count, width)
        grad_key = rotate(
            from_groups(key_share).reshape(row_count, head_count, 64), cosine_part, -sine_part
        ).reshape(row_count, width)
        grad_value = from_groups(value_share)
        grad_projected = jnp.concatenate([grad_query, grad_key, grad_value], axis=1).astype(jnp.bfloat16)
        joint_term = jnp.einsum("td,te->de", normed_in, grad_projected, preferred_element_type=jnp.float32)
        joint_offset_term = jnp.sum(grad_projected.astype(jnp.float32), axis=0)
        grad_in_norm = jnp.einsum("te,de->td", grad_projected, g_joint, preferred_element_type=jnp.float32)
        input_pull = jax.vjp(norm_rows, residual_in, in_gain, in_shift)[1]
        grad_first_in, input_gain_term, input_shift_term = input_pull(grad_in_norm)
        input_gradient = (grad_resid + grad_first_in)[None]
        (d_joint,) = reduce_params([joint_term])
        (
            d_in_gain,
            d_in_shift,
            d_joint_bias,
            d_out_bias,
            d_mid_gain,
            d_mid_shift,
            d_expand_bias,
            d_reduce_bias,
        ) = reduce_vectors(
            [
                input_gain_term,
                input_shift_term,
                joint_offset_term,
                output_offset_term,
                middle_gain_term,
                middle_shift_term,
                expand_offset_term,
                reduce_offset_term,
            ]
        )
        return (
            block_output,
            input_gradient,
            d_in_gain,
            d_in_shift,
            d_joint,
            d_joint_bias,
            d_out,
            d_out_bias,
            d_mid_gain,
            d_mid_shift,
            d_expand,
            d_expand_bias,
            d_reduce,
            d_reduce_bias,
        )

    return local


def solution(mesh):
    return jax.shard_map(
        make_local(mesh),
        mesh=mesh,
        in_specs=(
            P(("rep", "fsdp"), "seq", None),
            P(None, ("rep", "fsdp"), "seq"),
            P("fsdp"),
            P("fsdp"),
            P("fsdp", None),
            P("fsdp"),
            P("fsdp", None),
            P("fsdp"),
            P("fsdp"),
            P("fsdp"),
            P("fsdp", None),
            P("fsdp"),
            P("fsdp", None),
            P("fsdp"),
            P(("rep", "fsdp"), "seq", None),
        ),
        out_specs=(
            P(("rep", "fsdp"), "seq", None),
            P(("rep", "fsdp"), "seq", None),
            P("fsdp"),
            P("fsdp"),
            P("fsdp", None),
            P("fsdp"),
            P("fsdp", None),
            P("fsdp"),
            P("fsdp"),
            P("fsdp"),
            P("fsdp", None),
            P("fsdp"),
            P("fsdp", None),
            P("fsdp"),
        ),
        check_vma=False,
    )
```

```python
import jax
import jax.numpy as jnp
from jax import lax
from jax.sharding import PartitionSpec as P

epsilon = 1e-06
LEVEL = ("rep", "seq")
LANES = 128


def norm_rows(values, gains, shifts):
    average = jnp.mean(values, axis=-1, keepdims=True)
    centred = values - average
    spread = jnp.mean(centred * centred, axis=-1, keepdims=True)
    return centred * lax.rsqrt(spread + epsilon) * gains + shifts


def rotary_tables(positions):
    counter = jnp.arange(10).astype(jnp.float32)
    frequency = jnp.power(10000.0, -counter / 10.0)
    angles = positions.astype(jnp.float32)[:, :, None] * frequency
    angles = jnp.transpose(angles, (1, 0, 2))
    return (jnp.cos(angles), jnp.sin(angles))


def rotate(values, cosine_part, sine_part):
    length = values.shape[0]
    heads_count = values.shape[1]
    turned = values[:, :, :60].reshape(length, heads_count, 3, 2, 10)
    former = turned[:, :, :, 0, :]
    latter = turned[:, :, :, 1, :]
    cosine_wide = cosine_part[:, None, :, :]
    sine_wide = sine_part[:, None, :, :]
    new_former = former * cosine_wide - latter * sine_wide
    new_latter = latter * cosine_wide + former * sine_wide
    joined = jnp.stack([new_former, new_latter], axis=3).reshape(length, heads_count, 60)
    return jnp.concatenate([joined, values[:, :, 60:]], axis=2)


def exact_gelu(values):
    return jax.nn.gelu(values, approximate=False)


def split_heads(block):
    return block.reshape(block.shape[0], block.shape[1] // 64, 64)


def group_scores(query_heads, key_heads):
    return (
        jnp.einsum("thd,shd->hts", query_heads, key_heads, preferred_element_type=jnp.float32)
        * 0.125
    )


def attend(inputs):
    query_block, key_block, value_block = inputs
    query_heads = split_heads(query_block)
    key_heads = split_heads(key_block)
    value_heads = split_heads(value_block)
    scores = group_scores(query_heads, key_heads)
    row_max = jnp.max(scores, axis=2, keepdims=True)
    raised = jnp.exp(scores - row_max)
    row_total = jnp.sum(raised, axis=2, keepdims=True)
    probs_low = (raised / row_total).astype(jnp.bfloat16)
    mixed = jnp.einsum("hts,shd->thd", probs_low, value_heads, preferred_element_type=jnp.float32)
    return (mixed.reshape(query_block.shape[0], -1), row_max, row_total)


def attend_back(inputs):
    query_block, key_block, value_block, grad_block, row_max, row_total = inputs
    query_heads = split_heads(query_block)
    key_heads = split_heads(key_block)
    value_heads = split_heads(value_block)
    grad_heads = split_heads(grad_block)
    scores = group_scores(query_heads, key_heads)
    probs = jnp.exp(scores - row_max) / row_total
    probs_low = probs.astype(jnp.bfloat16)
    grad_probs = jnp.einsum(
        "thd,shd->hts", grad_heads, value_heads, preferred_element_type=jnp.float32
    )
    value_grad = jnp.einsum(
        "hts,thd->shd", probs_low, grad_heads, preferred_element_type=jnp.float32
    )
    inner = jnp.sum(grad_probs * probs, axis=2, keepdims=True)
    grad_scores = (probs * (grad_probs - inner)).astype(jnp.bfloat16)
    query_grad = (
        jnp.einsum("hts,shd->thd", grad_scores, key_heads, preferred_element_type=jnp.float32)
        * 0.125
    )
    key_grad = (
        jnp.einsum("hts,thd->shd", grad_scores, query_heads, preferred_element_type=jnp.float32)
        * 0.125
    )
    return (
        query_grad.reshape(query_block.shape[0], -1),
        key_grad.reshape(key_block.shape[0], -1),
        value_grad.reshape(key_block.shape[0], -1),
    )


def make_comm(mesh):
    n_rep, n_fsdp, n_seq = mesh.shape["rep"], mesh.shape["fsdp"], mesh.shape["seq"]
    level = n_rep * n_seq
    bits = level.bit_length() - 1
    assert 1 << bits == level and n_seq & (n_seq - 1) == 0 and n_rep % 2 == 0
    assert n_fsdp & (n_fsdp - 1) == 0
    x_bits = list(range(n_seq.bit_length() - 1))
    core_bit = len(x_bits)
    y_bits = list(range(core_bit + 1, bits))

    def level_index():
        return lax.axis_index("rep") * n_seq + lax.axis_index("seq")

    def flip(bit):
        return [(k, k ^ (1 << bit)) for k in range(level)]

    def gather(piece, lead, order=None):
        k = level_index()
        blocks = [(piece, 0)]
        for bit in order or (x_bits + y_bits + [core_bit]):
            blocks = blocks + [
                (lax.ppermute(block, LEVEL, flip(bit)), mask ^ (1 << bit)) for block, mask in blocks
            ]
        out = jnp.zeros((lead, level) + piece.shape[1:], piece.dtype)
        for block, mask in blocks:
            out = lax.dynamic_update_slice_in_dim(out, block[:, None], k ^ mask, axis=1)
        return out

    def reduce(total):
        k = level_index()
        lead = total.shape[0]
        acc = total.reshape((lead,) + (2,) * bits + total.shape[2:])
        alive = list(range(bits - 1, -1, -1))
        for bit in [core_bit] + y_bits[::-1] + x_bits[::-1]:
            axis = 1 + alive.index(bit)
            mine = (k >> bit) & 1
            keep = lax.dynamic_index_in_dim(acc, mine, axis, keepdims=False)
            send = lax.dynamic_index_in_dim(acc, 1 - mine, axis, keepdims=False)
            recv = lax.ppermute(send.astype(jnp.bfloat16), LEVEL, flip(bit))
            acc = keep.astype(jnp.float32) + recv.astype(jnp.float32)
            alive.remove(bit)
        return acc

    def line_reduce(acc):
        i = lax.axis_index("fsdp")
        n = n_fsdp
        up = [(a, a + 1) for a in range(n - 1)]
        down = [(a, a - 1) for a in range(1, n)]
        from_below = jnp.zeros(acc.shape[1:], jnp.float32)
        from_above = jnp.zeros(acc.shape[1:], jnp.float32)
        for step in range(1, n):
            j_up = jnp.clip(i + n - step, 0, n - 1)
            j_down = jnp.clip(i - (n - step), 0, n - 1)
            send_up = lax.dynamic_index_in_dim(acc, j_up, 0, keepdims=False) + from_below
            send_down = lax.dynamic_index_in_dim(acc, j_down, 0, keepdims=False) + from_above
            from_below = lax.ppermute(send_up.astype(jnp.bfloat16), "fsdp", up).astype(jnp.float32)
            from_above = lax.ppermute(send_down.astype(jnp.bfloat16), "fsdp", down).astype(jnp.float32)
        return lax.dynamic_index_in_dim(acc, i, 0, keepdims=False) + from_below + from_above

    def gather_weight(shard):
        rows, cols = shard.shape
        pieces = shard.reshape(level, rows // level, cols)
        mine = lax.dynamic_index_in_dim(pieces, level_index(), 0, keepdims=False)
        along = lax.all_gather(mine, "fsdp", axis=0, tiled=False)
        return gather(along, n_fsdp).reshape(n_fsdp * rows, cols)

    def reduce_weight(term):
        rows, cols = term.shape
        per = rows // (n_fsdp * level)
        acc = reduce(term.astype(jnp.bfloat16).reshape(n_fsdp, level, per, cols))
        share = line_reduce(acc).astype(jnp.bfloat16)
        full = gather(share[None], 1, y_bits + x_bits + [core_bit])
        return full.reshape(rows // n_fsdp, cols).astype(jnp.float32)

    def flat_piece(shard):
        rows, cols = shard.shape
        per = rows // level
        mine = lax.dynamic_index_in_dim(shard.reshape(level, per, cols), level_index(), 0, keepdims=False)
        return mine.reshape(per * cols // LANES, LANES)

    def gather_together(shards, vectors):
        parts = [flat_piece(s) for s in shards]
        lengths = [v.shape[0] for v in vectors]
        if vectors:
            vector_rows = -(-sum(lengths) // LANES)
            flat_vec = jnp.pad(jnp.concatenate(vectors), (0, vector_rows * LANES - sum(lengths)))
            parts.append(flat_vec.reshape(vector_rows, LANES))
        along = lax.all_gather(jnp.concatenate(parts, axis=0), "fsdp", axis=0, tiled=False)
        fulls = []
        at = 0
        for s, p in zip(shards, parts):
            rows, cols = s.shape
            piece = along[:, at : at + p.shape[0]].reshape(n_fsdp, rows // level, cols)
            fulls.append(gather(piece, n_fsdp).reshape(n_fsdp * rows, cols))
            at += p.shape[0]
        outs = []
        if vectors:
            vec_part = along[:, at:].reshape(n_fsdp, -1)
            pos = 0
            for length in lengths:
                outs.append(vec_part[:, pos : pos + length].reshape(-1))
                pos += length
        return fulls, outs

    def gather_vectors(shards):
        packed = jnp.concatenate(shards)
        full = lax.all_gather(packed, "fsdp", axis=0, tiled=False)
        outs = []
        at = 0
        for s in shards:
            outs.append(full[:, at : at + s.shape[0]].reshape(-1))
            at += s.shape[0]
        return outs

    def reduce_vectors(terms):
        total = jnp.concatenate(terms)
        for bit in range(bits):
            total = total + lax.ppermute(total, LEVEL, flip(bit))
        for bit in range(n_fsdp.bit_length() - 1):
            total = total + lax.ppermute(
                total, "fsdp", [(a, a ^ (1 << bit)) for a in range(n_fsdp)]
            )
        f = lax.axis_index("fsdp")
        outs = []
        at = 0
        for t in terms:
            own = t.shape[0] // n_fsdp
            outs.append(lax.dynamic_slice_in_dim(total, at + f * own, own))
            at += t.shape[0]
        return outs

    def gather_params(shards):
        return [gather_weight(s) if s.ndim == 2 else s for s in shards]

    def reduce_params(terms):
        return [reduce_weight(t) if t.ndim == 2 else t for t in terms]

    return gather_params, reduce_params, gather_together, reduce_vectors


def seq_swap(block, n_seq):
    if n_seq == 2:
        return lax.ppermute(block, "seq", [(0, 1), (1, 0)])
    raise NotImplementedError


def make_local(mesh):
    gather_params, reduce_params, gather_together, reduce_vectors = make_comm(mesh)
    n_seq = mesh.shape["seq"]

    def local(
        tokens,
        positions,
        input_gain,
        input_shift,
        joint_weight,
        joint_bias,
        output_weight,
        output_bias,
        middle_gain,
        middle_shift,
        expand_weight,
        expand_bias,
        reduce_weight,
        reduce_bias,
        cotangent,
    ):
        (g_joint,), (
            g_in_gain,
            g_in_shift,
            g_joint_bias,
            g_out_bias,
            g_mid_gain,
            g_mid_shift,
            g_expand_bias,
            g_reduce_bias,
        ) = gather_together(
            [joint_weight],
            [
                input_gain,
                input_shift,
                joint_bias,
                output_bias,
                middle_gain,
                middle_shift,
                expand_bias,
                reduce_bias,
            ],
        )
        (g_out, g_expand), _ = gather_together([output_weight, expand_weight], [])
        (g_reduce,) = gather_params([reduce_weight])

        row_count = tokens.shape[1]
        width = tokens.shape[2]
        head_count = width // 64
        per_group = min(4, head_count)
        group_count = head_count // per_group
        group_width = per_group * 64

        def to_groups(block):
            return jnp.transpose(block.reshape(block.shape[0], group_count, group_width), (1, 0, 2))

        def from_groups(block):
            return jnp.transpose(block, (1, 0, 2)).reshape(block.shape[1], width)

        residual_in = tokens[0].astype(jnp.float32)
        cosine_part, sine_part = rotary_tables(positions[:, 0, :])
        in_gain = g_in_gain.astype(jnp.float32)
        in_shift = g_in_shift.astype(jnp.float32)
        normed_in = norm_rows(residual_in, in_gain, in_shift).astype(jnp.bfloat16)
        projected = jnp.dot(normed_in, g_joint, preferred_element_type=jnp.float32) + g_joint_bias.astype(
            jnp.float32
        )
        queries = (
            rotate(projected[:, :width].reshape(row_count, head_count, 64), cosine_part, sine_part)
            .astype(jnp.bfloat16)
            .reshape(row_count, width)
        )
        keys = (
            rotate(
                projected[:, width : 2 * width].reshape(row_count, head_count, 64),
                cosine_part,
                sine_part,
            )
            .astype(jnp.bfloat16)
            .reshape(row_count, width)
        )
        values = projected[:, 2 * width :].astype(jnp.bfloat16)
        query_groups = to_groups(queries)
        key_mine = to_groups(keys)
        value_mine = to_groups(values)
        key_all = jnp.concatenate([key_mine, seq_swap(key_mine, n_seq)], axis=1)
        value_all = jnp.concatenate([value_mine, seq_swap(value_mine, n_seq)], axis=1)
        mixed, row_max, row_total = lax.map(attend, (query_groups, key_all, value_all))
        attended = from_groups(mixed).astype(jnp.bfloat16)
        residual_mid = residual_in + (
            jnp.dot(attended, g_out, preferred_element_type=jnp.float32) + g_out_bias.astype(jnp.float32)
        )
        mid_gain = g_mid_gain.astype(jnp.float32)
        mid_shift = g_mid_shift.astype(jnp.float32)
        normed_mid = norm_rows(residual_mid, mid_gain, mid_shift).astype(jnp.bfloat16)
        upper = jnp.dot(normed_mid, g_expand, preferred_element_type=jnp.float32) + g_expand_bias.astype(
            jnp.float32
        )
        hidden = exact_gelu(upper).astype(jnp.bfloat16)
        result = residual_mid + (
            jnp.dot(hidden, g_reduce, preferred_element_type=jnp.float32) + g_reduce_bias.astype(jnp.float32)
        )
        block_output = result.astype(jnp.bfloat16)[None]

        grad_low = cotangent[0]
        grad_out = grad_low.astype(jnp.float32)
        reduce_term = jnp.einsum("tf,td->fd", hidden, grad_low, preferred_element_type=jnp.float32)
        reduce_offset_term = jnp.sum(grad_out, axis=0)
        (d_reduce,) = reduce_params([reduce_term])
        grad_hidden = jnp.einsum("td,fd->tf", grad_low, g_reduce, preferred_element_type=jnp.float32)
        gelu_pull = jax.vjp(exact_gelu, upper)[1]
        grad_upper = gelu_pull(grad_hidden)[0].astype(jnp.bfloat16)
        expand_term = jnp.einsum("td,tf->df", normed_mid, grad_upper, preferred_element_type=jnp.float32)
        expand_offset_term = jnp.sum(grad_upper.astype(jnp.float32), axis=0)
        (d_expand,) = reduce_params([expand_term])
        grad_mid_norm = jnp.einsum("tf,df->td", grad_upper, g_expand, preferred_element_type=jnp.float32)
        middle_pull = jax.vjp(norm_rows, residual_mid, mid_gain, mid_shift)[1]
        grad_mid_in, middle_gain_term, middle_shift_term = middle_pull(grad_mid_norm)
        grad_resid = grad_out + grad_mid_in
        grad_branch = grad_resid.astype(jnp.bfloat16)
        output_term = jnp.einsum("td,te->de", attended, grad_branch, preferred_element_type=jnp.float32)
        output_offset_term = jnp.sum(grad_branch.astype(jnp.float32), axis=0)
        (d_out,) = reduce_params([output_term])
        grad_attended = jnp.einsum(
            "te,de->td", grad_branch, g_out, preferred_element_type=jnp.float32
        ).astype(jnp.bfloat16)
        query_grad, key_grad, value_grad = lax.map(
            attend_back,
            (query_groups, key_all, value_all, to_groups(grad_attended), row_max, row_total),
        )
        half = row_count
        key_share = key_grad[:, :half] + seq_swap(
            key_grad[:, half:].astype(jnp.bfloat16), n_seq
        ).astype(jnp.float32)
        value_share = value_grad[:, :half] + seq_swap(
            value_grad[:, half:].astype(jnp.bfloat16), n_seq
        ).astype(jnp.float32)
        grad_query = rotate(
            from_groups(query_grad).reshape(row_count, head_count, 64), cosine_part, -sine_part
        ).reshape(row_count, width)
        grad_key = rotate(
            from_groups(key_share).reshape(row_count, head_count, 64), cosine_part, -sine_part
        ).reshape(row_count, width)
        grad_value = from_groups(value_share)
        grad_projected = jnp.concatenate([grad_query, grad_key, grad_value], axis=1).astype(jnp.bfloat16)
        joint_term = jnp.einsum("td,te->de", normed_in, grad_projected, preferred_element_type=jnp.float32)
        joint_offset_term = jnp.sum(grad_projected.astype(jnp.float32), axis=0)
        grad_in_norm = jnp.einsum("te,de->td", grad_projected, g_joint, preferred_element_type=jnp.float32)
        input_pull = jax.vjp(norm_rows, residual_in, in_gain, in_shift)[1]
        grad_first_in, input_gain_term, input_shift_term = input_pull(grad_in_norm)
        input_gradient = (grad_resid + grad_first_in)[None]
        (d_joint,) = reduce_params([joint_term])
        (
            d_in_gain,
            d_in_shift,
            d_joint_bias,
            d_out_bias,
            d_mid_gain,
            d_mid_shift,
            d_expand_bias,
            d_reduce_bias,
        ) = reduce_vectors(
            [
                input_gain_term,
                input_shift_term,
                joint_offset_term,
                output_offset_term,
                middle_gain_term,
                middle_shift_term,
                expand_offset_term,
                reduce_offset_term,
            ]
        )
        return (
            block_output,
            input_gradient,
            d_in_gain,
            d_in_shift,
            d_joint,
            d_joint_bias,
            d_out,
            d_out_bias,
            d_mid_gain,
            d_mid_shift,
            d_expand,
            d_expand_bias,
            d_reduce,
            d_reduce_bias,
        )

    return local


def solution(mesh):
    return jax.shard_map(
        make_local(mesh),
        mesh=mesh,
        in_specs=(
            P(("rep", "fsdp"), "seq", None),
            P(None, ("rep", "fsdp"), "seq"),
            P("fsdp"),
            P("fsdp"),
            P("fsdp", None),
            P("fsdp"),
            P("fsdp", None),
            P("fsdp"),
            P("fsdp"),
            P("fsdp"),
            P("fsdp", None),
            P("fsdp"),
            P("fsdp", None),
            P("fsdp"),
            P(("rep", "fsdp"), "seq", None),
        ),
        out_specs=(
            P(("rep", "fsdp"), "seq", None),
            P(("rep", "fsdp"), "seq", None),
            P("fsdp"),
            P("fsdp"),
            P("fsdp", None),
            P("fsdp"),
            P("fsdp", None),
            P("fsdp"),
            P("fsdp"),
            P("fsdp"),
            P("fsdp", None),
            P("fsdp"),
            P("fsdp", None),
            P("fsdp"),
        ),
        check_vma=False,
    )
```
